512 devices in a mesh: lat: 32 (over z, core), lon: 16 (over x, y).
Axes of the slice: x: 4, y: 4, z: 16, core: 2. Of those that a mesh axis runs over, the one named last changes fastest.
Arguments:
- source: float32 [8, 1024, 2048], P(None, 'lat', 'lon'), may hold values from -6 to 6
- kappa_lon: bfloat16 [8, 1024, 2048], P(None, 'lat', 'lon'), may hold values from 32768 to 262144
- kappa_lat: bfloat16 [8, 1024, 2048], P(None, 'lat', 'lon'), may hold values from 2048 to 16384
- sea_mask: int32 [8, 1024, 2048], P(None, 'lat', 'lon'), may hold values 0 or 1
Outputs:
- analysis: float32 [8, 1024, 2048], P(None, 'lat', 'lon')
The draws below stay inside these ranges and needn't reach their ends.
All inputs are finite; a program needn't handle non-finite values. No bound on the sum of `sea_mask` on one device may be relied on, other than what follows from the above.
Results may differ from the reference program's by a relative error of at most 0.0003.
Values sent between devices are 32-bit elements; how exact they have to be, the bound alone decides.
No kernel may reach another device: no remote copies, remote signals or barrier semaphores. Data moves between devices by JAX's collectives and lax.ppermute only.
A program may use at most 64 MiB of HBM per device.

```python
import math
import jax
import jax.numpy as jnp
from jax import lax

LEV = 8
NLON = 2048
NLAT = 1024


def draw_source(key, part):
    shape = (LEV, NLAT, NLON)
    values = jnp.clip(jax.random.normal(key, shape, jnp.float32), -6.0, 6.0)
    return values


def plant(result, own_key, least, largest):
    spot = [jax.random.randint(jax.random.fold_in(own_key, axis), (), 0, length) for axis, length in enumerate(result.shape)]
    longest = result.shape.index(max(result.shape))
    next_to = spot[:longest] + [(spot[longest] + 1) % result.shape[longest]] + spot[longest + 1:]
    return result.at[tuple(spot)].set(least).at[tuple(next_to)].set(largest)


def block_levels(rng, extent, cuts, smallest, high):
    loudness, own = 1.0, jax.random.fold_in(rng, 6)
    for dim, parts in cuts:
        steps = jnp.exp(jax.random.uniform(jax.random.fold_in(own, dim), (parts,), jnp.float32, smallest / len(cuts), high / len(cuts)))
        loudness = loudness * jnp.repeat(steps, extent[dim] // parts).reshape([-1 if axis == dim else 1 for axis in range(len(extent))])
    return loudness


def setup_inputs(seed: int = 0) -> dict:
    arg_keys = jax.random.split(jax.random.key(seed), 5)
    source = draw_source(jax.random.fold_in(arg_keys[4], 71), 0)
    kappa_lon = jnp.clip(jnp.exp(math.log(262144.0) - 2.0794415 * jax.random.uniform(arg_keys[1], (LEV, NLAT, NLON), jnp.float32) ** block_levels(arg_keys[1], (LEV, NLAT, NLON), ((1, 32), (2, 16)), -0.2, 0.2)), 32768.0, 262144.0).astype(jnp.bfloat16)
    kappa_lat = jnp.clip(jnp.exp(math.log(16384.0) - 2.0794415 * jax.random.uniform(arg_keys[2], (LEV, NLAT, NLON), jnp.float32) ** block_levels(arg_keys[2], (LEV, NLAT, NLON), ((1, 32), (2, 16)), -0.2, 0.2)), 2048.0, 16384.0).astype(jnp.bfloat16)
    sea_mask = plant((jax.random.randint(arg_keys[3], (LEV, NLAT, NLON), 0, 256) < 255).astype(jnp.int32), jax.random.fold_in(arg_keys[3], 1), 0, 1)
    return {"source": source, "kappa_lon": kappa_lon, "kappa_lat": kappa_lat, "sea_mask": sea_mask}


def thomas(lower_band, upper_band, excess, sources):

    def forward(carried, entries):
        excess_prev, upper_prev, source_prev = carried
        lower_now, upper_now, excess_now, source_now = entries
        factor = lower_now / (excess_prev - upper_prev)
        excess_new = excess_now - factor * excess_prev
        source_new = source_now - factor * source_prev
        return ((excess_new, upper_now, source_new), (excess_new - upper_now, source_new))
    start = (jnp.ones_like(excess[0]), jnp.zeros_like(excess[0]), jnp.zeros_like(sources[0]))
    _, (pivots, reduced_system) = lax.scan(forward, start, (lower_band, upper_band, excess, sources))

    def backward(next_value, entries):
        pivot, source_now, upper_now = entries
        value = (source_now - upper_now * next_value) / pivot
        return (value, value)
    _, solved = lax.scan(backward, jnp.zeros_like(sources[0]), (pivots, reduced_system, upper_band), reverse=True)
    return solved

def periodic(left_face, right_face, values):
    length = values.shape[0]
    position = lax.broadcasted_iota(jnp.int32, values.shape, 0)
    lower_band = jnp.where(position == 0, 0.0, -left_face)
    upper_band = jnp.where(position == length - 2, 0.0, -right_face)
    excess = 1.0 + jnp.where(position == 0, left_face, 0.0) + jnp.where(position == length - 2, right_face, 0.0)
    inner = values[:-1]
    sources = jnp.stack([inner, jnp.ones_like(inner)], 1)
    solved = thomas(lower_band[:-1], upper_band[:-1], excess[:-1], sources)
    particular = solved[:, 0]
    deficit = solved[:, 1]
    lower_last = -left_face[length - 1]
    upper_last = -right_face[length - 1]
    last_value = (values[length - 1] - lower_last * particular[length - 2] - upper_last * particular[0]) / (1.0 - lower_last * deficit[length - 2] - upper_last * deficit[0])
    return jnp.concatenate([particular + (1.0 - deficit) * last_value, last_value[None]], 0)

def open_solve(left_face, right_face, values):
    solved = thomas(-left_face, -right_face, jnp.ones_like(values), values[:, None])
    return solved[:, 0]

def reference(source, kappa_lon, kappa_lat, sea_mask):
    wet_cells = sea_mask.astype(jnp.float32)
    lon_kappa = kappa_lon.astype(jnp.float32)
    lat_kappa = kappa_lat.astype(jnp.float32)
    lon_face = lon_kappa * wet_cells * jnp.roll(wet_cells, -1, 2)
    lon_left = jnp.roll(lon_face, 1, 2)
    lon_pass = jnp.moveaxis(periodic(jnp.moveaxis(lon_left, 2, 0), jnp.moveaxis(lon_face, 2, 0), jnp.moveaxis(source, 2, 0)), 0, 2)
    north_wet = jnp.concatenate([wet_cells[:, 1:], jnp.zeros_like(wet_cells[:, :1])], 1)
    lat_face = lat_kappa * wet_cells * north_wet
    lat_left = jnp.concatenate([jnp.zeros_like(lat_face[:, :1]), lat_face[:, :-1]], 1)
    lat_pass = jnp.moveaxis(open_solve(jnp.moveaxis(lat_left, 1, 0), jnp.moveaxis(lat_face, 1, 0), jnp.moveaxis(lon_pass, 1, 0)), 0, 1)
    return wet_cells * 4.0 * jnp.sqrt(jnp.sqrt(lon_kappa * lat_kappa)) * lat_pass
```

```python
import jax
import jax.numpy as jnp
from jax import lax
from jax.sharding import PartitionSpec as P


def padded(array, sides, width):
    for axis, dim in sides:
        peers, length = (lax.axis_size(axis), array.shape[dim])
        up = [(i, (i + 1) % peers) for i in range(peers)]
        down = [(j, i) for i, j in up]
        last = lax.slice_in_dim(array, length - width, length, axis=dim)
        leading = lax.slice_in_dim(array, 0, width, axis=dim)
        before = lax.ppermute(last, axis, up)
        after = lax.ppermute(leading, axis, down)
        array = jnp.concatenate([before, array, after], axis=dim)
    return array


def earlier(values, stride, axis):
    length = values.shape[axis]
    padding = jnp.zeros_like(lax.slice_in_dim(values, 0, stride, axis=axis))
    return jnp.concatenate([padding, lax.slice_in_dim(values, 0, length - stride, axis=axis)], axis)


def following(values, stride, axis):
    length = values.shape[axis]
    padding = jnp.zeros_like(lax.slice_in_dim(values, 0, stride, axis=axis))
    return jnp.concatenate([lax.slice_in_dim(values, stride, length, axis=axis), padding], axis)


def local_solve(lower_band, upper_band, excess, sources, axis):
    length = lower_band.shape[axis]
    stride = 1
    while stride < length:
        inverse = 1.0 / (excess - lower_band - upper_band)
        left_weight = -lower_band * earlier(inverse, stride, axis)
        right_coefficient = -upper_band * following(inverse, stride, axis)
        new_lower = left_weight * earlier(lower_band, stride, axis)
        new_upper = right_coefficient * following(upper_band, stride, axis)
        excess = (
            excess
            + left_weight * earlier(excess, stride, axis)
            + right_coefficient * following(excess, stride, axis)
        )
        sources = (
            sources
            + left_weight * earlier(sources, stride, axis + 1)
            + right_coefficient * following(sources, stride, axis + 1)
        )
        lower_band, upper_band = (new_lower, new_upper)
        stride = stride * 2
    return sources / (excess - lower_band - upper_band)


def reduced_from(own_terms, next_terms):
    coupling, own_source, own_excess, upper_end = own_terms
    next_particular, next_right, next_deficit = next_terms
    return (
        coupling,
        upper_end * next_right,
        own_excess - upper_end * next_deficit,
        own_source - upper_end * next_particular,
    )


def parallel_cyclic_reduction_update(tridiagonal_system, leading_terms, trailing_terms):
    lower_band, upper_band, excess, sources = tridiagonal_system
    lower_b, upper_b, excess_b, source_b = leading_terms
    lower_a, upper_a, excess_a, source_a = trailing_terms
    left_weight = -lower_band / (excess_b - lower_b - upper_b)
    right_coefficient = -upper_band / (excess_a - lower_a - upper_a)
    return (
        left_weight * lower_b,
        right_coefficient * upper_a,
        excess + left_weight * excess_b + right_coefficient * excess_a,
        sources + left_weight * source_b + right_coefficient * source_a,
    )


def circular_solve(tridiagonal_system):
    devices = tridiagonal_system[0].shape[0]
    stride = 1
    while stride < devices:
        leading_terms = tuple(
            (jnp.roll(ensemble_member, stride, 0) for ensemble_member in tridiagonal_system)
        )
        trailing_terms = tuple(
            (jnp.roll(ensemble_member, -stride, 0) for ensemble_member in tridiagonal_system)
        )
        tridiagonal_system = parallel_cyclic_reduction_update(
            tridiagonal_system, leading_terms, trailing_terms
        )
        stride = stride * 2
    return tridiagonal_system[3] / tridiagonal_system[2]


def gathered_solve(gathered, device_index):
    own_terms = gathered[:4]
    next_terms = tuple((jnp.roll(ensemble_member, -1, 0) for ensemble_member in gathered[4:]))
    interface = circular_solve(reduced_from(own_terms, next_terms))
    devices = interface.shape[0]
    here_value = lax.dynamic_index_in_dim(interface, device_index, 0, keepdims=False)
    before_value = lax.dynamic_index_in_dim(
        interface, (device_index + devices - 1) % devices, 0, keepdims=False
    )
    return (before_value, here_value)


def axis_gathered(own_terms, head_terms, axis):
    stacked = jnp.stack(tuple(own_terms) + tuple(head_terms), 0)
    gathered = lax.all_gather(stacked[None], axis, axis=0, tiled=True)
    gathered = tuple(gathered[:, k] for k in range(stacked.shape[0]))
    return gathered_solve(gathered, lax.axis_index(axis))


def lon_gathered(own_terms, head_terms):
    return axis_gathered(own_terms, head_terms, "lon")


def lat_gathered(own_terms, head_terms):
    return axis_gathered(own_terms, head_terms, "lat")


def line_pass(values, left_face, right_face, axis, reduce_edges):
    length = values.shape[axis]
    position = lax.broadcasted_iota(jnp.int32, values.shape, axis)
    is_first = position == 0
    is_last = position == length - 1
    is_penult = position == length - 2
    lower_band = jnp.where(is_first | is_last, 0.0, -left_face)
    upper_band = jnp.where(is_penult | is_last, 0.0, -right_face)
    excess = 1.0 + jnp.where(is_first, left_face, 0.0) + jnp.where(is_penult, right_face, 0.0)
    sources = jnp.stack(
        [
            jnp.where(is_last, 0.0, values),
            jnp.where(is_first, left_face, 0.0),
            jnp.where(is_penult, right_face, 0.0) + jnp.where(is_last, 1.0, 0.0),
            jnp.where(is_last, 0.0, 1.0),
        ],
        0,
    )
    solved = local_solve(lower_band, upper_band, excess, sources, axis)
    particular, from_left, right_contribution, deficit = (
        solved[0],
        solved[1],
        solved[2],
        solved[3],
    )

    def row_at(ensemble_member, place):
        return lax.index_in_dim(ensemble_member, place, axis, keepdims=False)

    lower_end = -row_at(left_face, length - 1)
    upper_end = -row_at(right_face, length - 1)
    own_terms = (
        lower_end * row_at(from_left, length - 2),
        row_at(values, length - 1) - lower_end * row_at(particular, length - 2),
        1.0 - lower_end * row_at(deficit, length - 2),
        upper_end,
    )
    head_terms = (row_at(particular, 0), row_at(right_contribution, 0), row_at(deficit, 0))
    before_value, here_value = reduce_edges(own_terms, head_terms)
    return (
        particular
        + from_left * jnp.expand_dims(before_value, axis)
        + right_contribution * jnp.expand_dims(here_value, axis)
    )


def shards(source, kappa_lon, kappa_lat, sea_mask):
    wet_cells = sea_mask.astype(jnp.float32)
    lon_kappa = kappa_lon.astype(jnp.float32)
    lat_kappa = kappa_lat.astype(jnp.float32)
    wet_pad, lon_pad, lat_pad = (
        padded(wet_cells, (("lat", 1), ("lon", 2)), 1),
        padded(lon_kappa, (("lat", 1), ("lon", 2)), 1),
        padded(lat_kappa, (("lat", 1), ("lon", 2)), 1),
    )
    lon_wet = wet_pad[:, 1:-1, :]
    lon_faces = lon_pad[:, 1:-1, :-1] * lon_wet[:, :, :-1] * lon_wet[:, :, 1:]
    lon_pass = line_pass(source, lon_faces[:, :, :-1], lon_faces[:, :, 1:], 2, lon_gathered)
    lat_wet = wet_pad[:, :, 1:-1]
    lat_faces = lat_pad[:, :-1, 1:-1] * lat_wet[:, :-1, :] * lat_wet[:, 1:, :]
    device_index = lax.axis_index("lat")
    devices = lax.axis_size("lat")
    position = lax.broadcasted_iota(jnp.int32, lat_faces.shape, 1)
    outer_face = (position == 0) & (device_index == 0) | (position == lat_faces.shape[1] - 1) & (
        device_index == devices - 1
    )
    lat_faces = jnp.where(outer_face, 0.0, lat_faces)
    lat_pass = line_pass(lon_pass, lat_faces[:, :-1, :], lat_faces[:, 1:, :], 1, lat_gathered)
    return wet_cells * 4.0 * jnp.sqrt(jnp.sqrt(lon_kappa * lat_kappa)) * lat_pass


def solution(mesh):
    return jax.shard_map(
        shards,
        mesh=mesh,
        in_specs=(
            P(None, "lat", "lon"),
            P(None, "lat", "lon"),
            P(None, "lat", "lon"),
            P(None, "lat", "lon"),
        ),
        out_specs=P(None, "lat", "lon"),
        check_vma=False,
    )
```

```python
import jax
import jax.numpy as jnp
from jax import lax
from jax.sharding import PartitionSpec as P


def earlier(values, stride, axis):
    length = values.shape[axis]
    padding = jnp.zeros_like(lax.slice_in_dim(values, 0, stride, axis=axis))
    return jnp.concatenate([padding, lax.slice_in_dim(values, 0, length - stride, axis=axis)], axis)


def following(values, stride, axis):
    length = values.shape[axis]
    padding = jnp.zeros_like(lax.slice_in_dim(values, 0, stride, axis=axis))
    return jnp.concatenate([lax.slice_in_dim(values, stride, length, axis=axis), padding], axis)


def local_solve(lower_band, upper_band, excess, sources, axis):
    length = lower_band.shape[axis]
    stride = 1
    while stride < length:
        inverse = 1.0 / (excess - lower_band - upper_band)
        left_weight = -lower_band * earlier(inverse, stride, axis)
        right_coefficient = -upper_band * following(inverse, stride, axis)
        new_lower = left_weight * earlier(lower_band, stride, axis)
        new_upper = right_coefficient * following(upper_band, stride, axis)
        excess = (
            excess
            + left_weight * earlier(excess, stride, axis)
            + right_coefficient * following(excess, stride, axis)
        )
        sources = (
            sources
            + left_weight * earlier(sources, stride, axis + 1)
            + right_coefficient * following(sources, stride, axis + 1)
        )
        lower_band, upper_band = (new_lower, new_upper)
        stride = stride * 2
    return sources / (excess - lower_band - upper_band)


def circular_solve(lower_band, upper_band, excess, sources):
    devices = lower_band.shape[0]
    stride = 1
    while stride < devices:
        inverse = 1.0 / (excess - lower_band - upper_band)
        left_weight = -lower_band * jnp.roll(inverse, stride, 0)
        right_coefficient = -upper_band * jnp.roll(inverse, -stride, 0)
        new_lower = left_weight * jnp.roll(lower_band, stride, 0)
        new_upper = right_coefficient * jnp.roll(upper_band, -stride, 0)
        excess = (
            excess
            + left_weight * jnp.roll(excess, stride, 0)
            + right_coefficient * jnp.roll(excess, -stride, 0)
        )
        sources = (
            sources
            + left_weight * jnp.roll(sources, stride, 0)
            + right_coefficient * jnp.roll(sources, -stride, 0)
        )
        lower_band, upper_band = (new_lower, new_upper)
        stride = stride * 2
    return sources / excess


def line_pass(values, faces, edge_kappa, edge_wet, axis, mesh_axis, periodic):
    length = values.shape[axis]
    position = lax.broadcasted_iota(jnp.int32, values.shape, axis)
    zero = jnp.zeros_like(lax.slice_in_dim(values, 0, 1, axis=axis))
    left_face = jnp.concatenate([zero, faces], axis)
    right_face = jnp.concatenate([faces, zero], axis)
    sources = jnp.stack(
        [
            values,
            jnp.where(position == 0, 1.0, 0.0),
            jnp.where(position == length - 1, 1.0, 0.0),
        ],
        0,
    )
    solved = local_solve(-left_face, -right_face, jnp.ones_like(values), sources, axis)
    particular, from_left, from_right = solved[0], solved[1], solved[2]

    def row_at(member, place):
        return lax.index_in_dim(member, place, axis, keepdims=False)

    terms = jnp.stack(
        [
            row_at(particular, 0),
            row_at(from_left, 0),
            row_at(from_right, 0),
            row_at(particular, length - 1),
            row_at(from_left, length - 1),
            row_at(from_right, length - 1),
            edge_kappa,
            edge_wet,
        ],
        0,
    )
    gathered = lax.all_gather(terms[None], mesh_axis, axis=0, tiled=True)
    head_p, head_u, head_w, tail_p, tail_u, tail_w, tail_kappa, head_wet = (
        gathered[:, k] for k in range(terms.shape[0])
    )
    devices = gathered.shape[0]

    def next_of(member):
        return jnp.roll(member, -1, 0)

    face = tail_kappa * next_of(head_wet)
    if not periodic:
        device = lax.broadcasted_iota(jnp.int32, face.shape, 0)
        face = jnp.where(device == devices - 1, 0.0, face)
    lower = -face * tail_u
    upper = -face * next_of(head_w)
    diagonal = 1.0 + face * (next_of(head_u) + tail_w)
    flux = circular_solve(lower, upper, diagonal + lower + upper, face * (next_of(head_p) - tail_p))
    index = lax.axis_index(mesh_axis)
    here = lax.dynamic_index_in_dim(flux, index, 0, keepdims=False)
    before = lax.dynamic_index_in_dim(flux, (index + devices - 1) % devices, 0, keepdims=False)
    return (
        particular
        - from_left * jnp.expand_dims(before, axis)
        + from_right * jnp.expand_dims(here, axis)
    )


def shards(source, kappa_lon, kappa_lat, sea_mask):
    wet_cells = sea_mask.astype(jnp.float32)
    lon_kappa = kappa_lon.astype(jnp.float32)
    lat_kappa = kappa_lat.astype(jnp.float32)
    lon_weight = lon_kappa * wet_cells
    lat_weight = lat_kappa * wet_cells
    lon_faces = lon_weight[:, :, :-1] * wet_cells[:, :, 1:]
    lon_pass = line_pass(
        source, lon_faces, lon_weight[:, :, -1], wet_cells[:, :, 0], 2, "lon", True
    )
    lat_faces = lat_weight[:, :-1, :] * wet_cells[:, 1:, :]
    lat_pass = line_pass(
        lon_pass, lat_faces, lat_weight[:, -1, :], wet_cells[:, 0, :], 1, "lat", False
    )
    return wet_cells * 4.0 * jnp.sqrt(jnp.sqrt(lon_kappa * lat_kappa)) * lat_pass


def solution(mesh):
    return jax.shard_map(
        shards,
        mesh=mesh,
        in_specs=(
            P(None, "lat", "lon"),
            P(None, "lat", "lon"),
            P(None, "lat", "lon"),
            P(None, "lat", "lon"),
        ),
        out_specs=P(None, "lat", "lon"),
        check_vma=False,
    )
```

```python
import functools

import jax
import jax.numpy as jnp
from jax import lax
from jax.experimental import pallas as pl
from jax.experimental.pallas import tpu as pltpu
from jax.sharding import PartitionSpec as P

TERMS = 7


def shifted(values, shift, axis):
    length = values.shape[axis]
    return pltpu.roll(values, shift % length, axis)


def block_solve(lower_band, upper_band, excess, sources, axis):
    length = lower_band.shape[axis]
    stride = 1
    while stride < length:
        inverse = 1.0 / (excess - lower_band - upper_band)
        left_weight = -lower_band * shifted(inverse, stride, axis)
        right_coefficient = -upper_band * shifted(inverse, -stride, axis)
        new_lower = left_weight * shifted(lower_band, stride, axis)
        new_upper = right_coefficient * shifted(upper_band, -stride, axis)
        excess = (
            excess
            + left_weight * shifted(excess, stride, axis)
            + right_coefficient * shifted(excess, -stride, axis)
        )
        sources = [
            member
            + left_weight * shifted(member, stride, axis)
            + right_coefficient * shifted(member, -stride, axis)
            for member in sources
        ]
        lower_band, upper_band = (new_lower, new_upper)
        stride = stride * 2
    diagonal = excess - lower_band - upper_band
    return [member / diagonal for member in sources]


def pass_kernel(axis, corrected, *refs):
    if corrected:
        (p_ref, u_ref, w_ref, before_ref, here_ref, kappa_ref, mask_ref,
         p_out, u_out, w_out, edge_out) = refs
        values = (
            p_ref[...]
            - u_ref[...] * before_ref[...]
            + w_ref[...] * here_ref[...]
        )
    else:
        (source_ref, kappa_ref, mask_ref, p_out, u_out, w_out, edge_out) = refs
        values = source_ref[...]
    shape = values.shape
    length = shape[axis]
    wet = mask_ref[...].astype(jnp.float32)
    weight = kappa_ref[...].astype(jnp.float32) * wet
    position = lax.broadcasted_iota(jnp.int32, shape, axis)
    last = position == length - 1
    right_face = jnp.where(last, 0.0, weight * shifted(wet, -1, axis))
    left_face = shifted(right_face, 1, axis)
    first = position == 0
    particular, from_left, from_right = block_solve(
        -left_face,
        -right_face,
        jnp.ones(shape, jnp.float32),
        [values, jnp.where(first, 1.0, 0.0), jnp.where(last, 1.0, 0.0)],
        axis,
    )
    p_out[...] = particular
    u_out[...] = from_left
    w_out[...] = from_right
    tail_weight = shifted(weight, 4, axis)
    entries = [
        wet * particular,
        shifted(wet * from_left, 1, axis),
        shifted(wet * from_right, 2, axis),
        tail_weight,
        shifted(from_left, 4 + 1, axis),
        shifted(from_right, 4 + 2, axis),
        shifted(particular, 4 + 3, axis),
    ]
    edge = entries[0]
    for k in range(1, TERMS):
        edge = jnp.where(position == k, entries[k], edge)
    if axis == 2:
        edge_out[...] = edge
    else:
        edge_out[...] = lax.slice_in_dim(edge, 0, 8, axis=axis)


def local_pass(axis, inputs):
    shape = inputs[0].shape
    corrected = len(inputs) > 3
    edge_shape = shape if axis == 2 else shape[:axis] + (8,) + shape[axis + 1:]
    return pl.pallas_call(
        functools.partial(pass_kernel, axis, corrected),
        out_shape=(
            jax.ShapeDtypeStruct(shape, jnp.float32),
            jax.ShapeDtypeStruct(shape, jnp.float32),
            jax.ShapeDtypeStruct(shape, jnp.float32),
            jax.ShapeDtypeStruct(edge_shape, jnp.float32),
        ),
    )(*inputs)


def circular_solve(lower_band, upper_band, excess, sources):
    devices = lower_band.shape[0]
    stride = 1
    while stride < devices:
        inverse = 1.0 / (excess - lower_band - upper_band)
        left_weight = -lower_band * jnp.roll(inverse, stride, 0)
        right_coefficient = -upper_band * jnp.roll(inverse, -stride, 0)
        new_lower = left_weight * jnp.roll(lower_band, stride, 0)
        new_upper = right_coefficient * jnp.roll(upper_band, -stride, 0)
        excess = (
            excess
            + left_weight * jnp.roll(excess, stride, 0)
            + right_coefficient * jnp.roll(excess, -stride, 0)
        )
        sources = (
            sources
            + left_weight * jnp.roll(sources, stride, 0)
            + right_coefficient * jnp.roll(sources, -stride, 0)
        )
        lower_band, upper_band = (new_lower, new_upper)
        stride = stride * 2
    return sources / excess


def interface_flux(edge, axis, mesh_axis, periodic):
    terms = lax.slice_in_dim(edge, 0, TERMS, axis=axis)
    gathered = lax.all_gather(terms[None], mesh_axis, axis=0, tiled=True)
    devices = gathered.shape[0]
    (head_p, head_u, head_w, tail_kappa, tail_u, tail_w, tail_p) = (
        lax.index_in_dim(gathered, k, axis + 1, keepdims=False) for k in range(TERMS)
    )

    def next_of(member):
        return jnp.roll(member, -1, 0)

    next_wet = jnp.where(next_of(head_u) > 0.0, 1.0, 0.0)
    face = tail_kappa * next_wet
    if not periodic:
        device = lax.broadcasted_iota(jnp.int32, face.shape, 0)
        face = jnp.where(device == devices - 1, 0.0, face)
        tail_kappa = jnp.where(device == devices - 1, 0.0, tail_kappa)
    lower = -face * tail_u
    upper = -tail_kappa * next_of(head_w)
    diagonal = 1.0 + tail_kappa * next_of(head_u) + face * tail_w
    flux = circular_solve(
        lower, upper, diagonal + lower + upper, tail_kappa * next_of(head_p) - face * tail_p
    )
    index = lax.axis_index(mesh_axis)
    here = lax.dynamic_index_in_dim(flux, index, 0, keepdims=True)
    before = lax.dynamic_index_in_dim(flux, (index + devices - 1) % devices, 0, keepdims=True)
    return before[0], here[0]


def shards(source, kappa_lon, kappa_lat, sea_mask):
    p_lon, u_lon, w_lon, edge_lon = local_pass(2, (source, kappa_lon, sea_mask))
    before, here = interface_flux(edge_lon, 2, "lon", True)
    p_lat, u_lat, w_lat, edge_lat = local_pass(
        1, (p_lon, u_lon, w_lon, before[:, :, None], here[:, :, None], kappa_lat, sea_mask)
    )
    before, here = interface_flux(edge_lat, 1, "lat", False)
    lat_pass = p_lat - u_lat * before[:, None, :] + w_lat * here[:, None, :]
    wet_cells = sea_mask.astype(jnp.float32)
    lon_kappa = kappa_lon.astype(jnp.float32)
    lat_kappa = kappa_lat.astype(jnp.float32)
    return wet_cells * 4.0 * jnp.sqrt(jnp.sqrt(lon_kappa * lat_kappa)) * lat_pass


def solution(mesh):
    return jax.shard_map(
        shards,
        mesh=mesh,
        in_specs=(
            P(None, "lat", "lon"),
            P(None, "lat", "lon"),
            P(None, "lat", "lon"),
            P(None, "lat", "lon"),
        ),
        out_specs=P(None, "lat", "lon"),
        check_vma=False,
    )
```

```python
import functools

import jax
import jax.numpy as jnp
from jax import lax
from jax.experimental import pallas as pl
from jax.experimental.pallas import tpu as pltpu
from jax.sharding import PartitionSpec as P

TERMS = 7


def shifted(values, shift, axis):
    length = values.shape[axis]
    return pltpu.roll(values, shift % length, axis)


def block_solve(lower_band, upper_band, excess, sources, axis):
    length = lower_band.shape[axis]
    stride = 1
    while stride < length:
        inverse = 1.0 / (excess - lower_band - upper_band)
        left_weight = -lower_band * shifted(inverse, stride, axis)
        right_coefficient = -upper_band * shifted(inverse, -stride, axis)
        new_lower = left_weight * shifted(lower_band, stride, axis)
        new_upper = right_coefficient * shifted(upper_band, -stride, axis)
        excess = (
            excess
            + left_weight * shifted(excess, stride, axis)
            + right_coefficient * shifted(excess, -stride, axis)
        )
        sources = [
            member
            + left_weight * shifted(member, stride, axis)
            + right_coefficient * shifted(member, -stride, axis)
            for member in sources
        ]
        lower_band, upper_band = (new_lower, new_upper)
        stride = stride * 2
    diagonal = excess - lower_band - upper_band
    return [member / diagonal for member in sources]


def pass_kernel(axis, corrected, *refs):
    if corrected:
        (p_ref, u_ref, w_ref, before_ref, here_ref, kappa_ref, mask_ref,
         p_out, u_out, w_out, edge_out) = refs
        values = (
            p_ref[...]
            - u_ref[...] * before_ref[...]
            + w_ref[...] * here_ref[...]
        )
    else:
        (source_ref, kappa_ref, mask_ref, p_out, u_out, w_out, edge_out) = refs
        values = source_ref[...]
    shape = values.shape
    length = shape[axis]
    wet = mask_ref[...].astype(jnp.float32)
    weight = kappa_ref[...].astype(jnp.float32) * wet
    position = lax.broadcasted_iota(jnp.int32, shape, axis)
    last = position == length - 1
    right_face = jnp.where(last, 0.0, weight * shifted(wet, -1, axis))
    left_face = shifted(right_face, 1, axis)
    first = position == 0
    particular, from_left, from_right = block_solve(
        -left_face,
        -right_face,
        jnp.ones(shape, jnp.float32),
        [values, jnp.where(first, 1.0, 0.0), jnp.where(last, 1.0, 0.0)],
        axis,
    )
    p_out[...] = particular
    u_out[...] = from_left
    w_out[...] = from_right
    tail_weight = shifted(weight, 4, axis)
    entries = [
        wet * particular,
        shifted(wet * from_left, 1, axis),
        shifted(wet * from_right, 2, axis),
        tail_weight,
        shifted(from_left, 4 + 1, axis),
        shifted(from_right, 4 + 2, axis),
        shifted(particular, 4 + 3, axis),
    ]
    edge = entries[0]
    for k in range(1, TERMS):
        edge = jnp.where(position == k, entries[k], edge)
    if axis == 2:
        edge_out[...] = edge
    else:
        edge_out[...] = lax.slice_in_dim(edge, 0, 8, axis=axis)


def local_pass(axis, inputs):
    shape = inputs[0].shape
    corrected = len(inputs) > 3
    edge_shape = shape if axis == 2 else shape[:axis] + (8,) + shape[axis + 1:]
    return pl.pallas_call(
        functools.partial(pass_kernel, axis, corrected),
        out_shape=(
            jax.ShapeDtypeStruct(shape, jnp.float32),
            jax.ShapeDtypeStruct(shape, jnp.float32),
            jax.ShapeDtypeStruct(shape, jnp.float32),
            jax.ShapeDtypeStruct(edge_shape, jnp.float32),
        ),
    )(*inputs)


def circular_solve(lower_band, upper_band, excess, sources):
    devices = lower_band.shape[0]
    stride = 1
    while stride < devices:
        inverse = 1.0 / (excess - lower_band - upper_band)
        left_weight = -lower_band * jnp.roll(inverse, stride, 0)
        right_coefficient = -upper_band * jnp.roll(inverse, -stride, 0)
        new_lower = left_weight * jnp.roll(lower_band, stride, 0)
        new_upper = right_coefficient * jnp.roll(upper_band, -stride, 0)
        excess = (
            excess
            + left_weight * jnp.roll(excess, stride, 0)
            + right_coefficient * jnp.roll(excess, -stride, 0)
        )
        sources = (
            sources
            + left_weight * jnp.roll(sources, stride, 0)
            + right_coefficient * jnp.roll(sources, -stride, 0)
        )
        lower_band, upper_band = (new_lower, new_upper)
        stride = stride * 2
    return sources / excess


def interface_flux(edge, axis, mesh_axis, periodic, exchange):
    terms = lax.slice_in_dim(edge, 0, TERMS, axis=axis)
    devices = lax.axis_size(mesh_axis)
    if exchange == "all_to_all":
        copies = jnp.broadcast_to(terms[None], (devices,) + terms.shape)
        gathered = lax.all_to_all(copies, mesh_axis, 0, 0, tiled=True)
    else:
        gathered = lax.all_gather(terms[None], mesh_axis, axis=0, tiled=True)
    (head_p, head_u, head_w, tail_kappa, tail_u, tail_w, tail_p) = (
        lax.index_in_dim(gathered, k, axis + 1, keepdims=False) for k in range(TERMS)
    )

    def next_of(member):
        return jnp.roll(member, -1, 0)

    next_wet = jnp.where(next_of(head_u) > 0.0, 1.0, 0.0)
    face = tail_kappa * next_wet
    if not periodic:
        device = lax.broadcasted_iota(jnp.int32, face.shape, 0)
        face = jnp.where(device == devices - 1, 0.0, face)
        tail_kappa = jnp.where(device == devices - 1, 0.0, tail_kappa)
    lower = -face * tail_u
    upper = -tail_kappa * next_of(head_w)
    diagonal = 1.0 + tail_kappa * next_of(head_u) + face * tail_w
    flux = circular_solve(
        lower, upper, diagonal + lower + upper, tail_kappa * next_of(head_p) - face * tail_p
    )
    index = lax.axis_index(mesh_axis)
    here = lax.dynamic_index_in_dim(flux, index, 0, keepdims=True)
    before = lax.dynamic_index_in_dim(flux, (index + devices - 1) % devices, 0, keepdims=True)
    return before[0], here[0]


def shards(source, kappa_lon, kappa_lat, sea_mask):
    p_lon, u_lon, w_lon, edge_lon = local_pass(2, (source, kappa_lon, sea_mask))
    before, here = interface_flux(edge_lon, 2, "lon", True, "all_to_all")
    p_lat, u_lat, w_lat, edge_lat = local_pass(
        1, (p_lon, u_lon, w_lon, before[:, :, None], here[:, :, None], kappa_lat, sea_mask)
    )
    before, here = interface_flux(edge_lat, 1, "lat", False, "all_gather")
    lat_pass = p_lat - u_lat * before[:, None, :] + w_lat * here[:, None, :]
    wet_cells = sea_mask.astype(jnp.float32)
    lon_kappa = kappa_lon.astype(jnp.float32)
    lat_kappa = kappa_lat.astype(jnp.float32)
    return wet_cells * 4.0 * jnp.sqrt(jnp.sqrt(lon_kappa * lat_kappa)) * lat_pass


def solution(mesh):
    return jax.shard_map(
        shards,
        mesh=mesh,
        in_specs=(
            P(None, "lat", "lon"),
            P(None, "lat", "lon"),
            P(None, "lat", "lon"),
            P(None, "lat", "lon"),
        ),
        out_specs=P(None, "lat", "lon"),
        check_vma=False,
    )
```

```python
import functools

import jax
import jax.numpy as jnp
from jax import lax
from jax.experimental import pallas as pl
from jax.experimental.pallas import tpu as pltpu
from jax.sharding import PartitionSpec as P

TERMS = 7


def shifted(values, shift, axis):
    length = values.shape[axis]
    return pltpu.roll(values, shift % length, axis)


def block_solve(lower_band, upper_band, excess, sources, axis, weights=None):
    length = lower_band.shape[axis]
    stride = 1
    while stride < length:
        inverse = 1.0 / (excess - lower_band - upper_band)
        left_weight = -lower_band * shifted(inverse, stride, axis)
        right_coefficient = -upper_band * shifted(inverse, -stride, axis)
        if weights is not None:
            weights.append((left_weight, right_coefficient))
        new_lower = left_weight * shifted(lower_band, stride, axis)
        new_upper = right_coefficient * shifted(upper_band, -stride, axis)
        excess = (
            excess
            + left_weight * shifted(excess, stride, axis)
            + right_coefficient * shifted(excess, -stride, axis)
        )
        sources = [
            member
            + left_weight * shifted(member, stride, axis)
            + right_coefficient * shifted(member, -stride, axis)
            for member in sources
        ]
        lower_band, upper_band = (new_lower, new_upper)
        stride = stride * 2
    diagonal = excess - lower_band - upper_band
    if weights is not None:
        weights.append(diagonal)
    return [member / diagonal for member in sources]


def pass_kernel(axis, corrected, *refs):
    if corrected:
        (p_ref, u_ref, w_ref, before_ref, here_ref, kappa_ref, mask_ref,
         p_out, u_out, w_out, edge_out) = refs
        values = (
            p_ref[...]
            - u_ref[...] * before_ref[...]
            + w_ref[...] * here_ref[...]
        )
    else:
        (source_ref, kappa_ref, mask_ref, p_out, u_out, w_out, edge_out) = refs
        values = source_ref[...]
    shape = values.shape
    length = shape[axis]
    wet = mask_ref[...].astype(jnp.float32)
    weight = kappa_ref[...].astype(jnp.float32) * wet
    position = lax.broadcasted_iota(jnp.int32, shape, axis)
    last = position == length - 1
    right_face = jnp.where(last, 0.0, weight * shifted(wet, -1, axis))
    left_face = shifted(right_face, 1, axis)
    first = position == 0
    particular, from_left, from_right = block_solve(
        -left_face,
        -right_face,
        jnp.ones(shape, jnp.float32),
        [values, jnp.where(first, 1.0, 0.0), jnp.where(last, 1.0, 0.0)],
        axis,
    )
    p_out[...] = particular
    u_out[...] = from_left
    w_out[...] = from_right
    tail_weight = shifted(weight, 4, axis)
    entries = [
        wet * particular,
        shifted(wet * from_left, 1, axis),
        shifted(wet * from_right, 2, axis),
        tail_weight,
        shifted(from_left, 4 + 1, axis),
        shifted(from_right, 4 + 2, axis),
        shifted(particular, 4 + 3, axis),
    ]
    edge = entries[0]
    for k in range(1, TERMS):
        edge = jnp.where(position == k, entries[k], edge)
    if axis == 2:
        edge_out[...] = edge
    else:
        edge_out[...] = lax.slice_in_dim(edge, 0, 8, axis=axis)


def local_pass(axis, inputs):
    shape = inputs[0].shape
    corrected = len(inputs) > 3
    edge_shape = shape if axis == 2 else shape[:axis] + (8,) + shape[axis + 1:]
    return pl.pallas_call(
        functools.partial(pass_kernel, axis, corrected),
        out_shape=(
            jax.ShapeDtypeStruct(shape, jnp.float32),
            jax.ShapeDtypeStruct(shape, jnp.float32),
            jax.ShapeDtypeStruct(shape, jnp.float32),
            jax.ShapeDtypeStruct(edge_shape, jnp.float32),
        ),
    )(*inputs)


def lat_matrix_kernel(kappa_ref, mask_ref, lon_kappa_ref, u_out, w_out, left_out, right_out,
                      diagonal_out, edge_out, scale_out):
    axis = 1
    wet = mask_ref[...].astype(jnp.float32)
    lat_kappa = kappa_ref[...].astype(jnp.float32)
    scale_out[...] = wet * 4.0 * jnp.sqrt(jnp.sqrt(lon_kappa_ref[...].astype(jnp.float32) * lat_kappa))
    weight = lat_kappa * wet
    shape = wet.shape
    length = shape[axis]
    position = lax.broadcasted_iota(jnp.int32, shape, axis)
    last = position == length - 1
    right_face = jnp.where(last, 0.0, weight * shifted(wet, -1, axis))
    left_face = shifted(right_face, 1, axis)
    weights = []
    from_left, from_right = block_solve(
        -left_face,
        -right_face,
        jnp.ones(shape, jnp.float32),
        [jnp.where(position == 0, 1.0, 0.0), jnp.where(last, 1.0, 0.0)],
        axis,
        weights,
    )
    u_out[...] = from_left
    w_out[...] = from_right
    for step, (left_weight, right_coefficient) in enumerate(weights[:-1]):
        left_out[step] = left_weight
        right_out[step] = right_coefficient
    diagonal_out[...] = weights[-1]
    entries = [
        None,
        shifted(wet * from_left, 1, axis),
        shifted(wet * from_right, 2, axis),
        shifted(weight, 4, axis),
        shifted(from_left, 4 + 1, axis),
        shifted(from_right, 4 + 2, axis),
    ]
    edge = entries[1]
    for k in range(2, 6):
        edge = jnp.where(position == k, entries[k], edge)
    edge_out[...] = lax.slice_in_dim(edge, 0, 8, axis=axis)


def lat_rhs_kernel(p_ref, u_ref, w_ref, before_ref, here_ref, mask_ref, left_ref, right_ref,
                   diagonal_ref, matrix_edge_ref, p_out, edge_out):
    axis = 1
    values = p_ref[...] - u_ref[...] * before_ref[...] + w_ref[...] * here_ref[...]
    length = values.shape[axis]
    stride = 1
    step = 0
    while stride < length:
        values = (
            values
            + left_ref[step] * shifted(values, stride, axis)
            + right_ref[step] * shifted(values, -stride, axis)
        )
        stride = stride * 2
        step = step + 1
    particular = values / diagonal_ref[...]
    p_out[...] = particular
    wet = mask_ref[...].astype(jnp.float32)
    position = lax.broadcasted_iota(jnp.int32, values.shape, axis)
    edge = jnp.where(position == 0, wet * particular, shifted(particular, 4 + 3, axis))
    edge = lax.slice_in_dim(edge, 0, 8, axis=axis)
    row = lax.broadcasted_iota(jnp.int32, edge.shape, axis)
    edge_out[...] = jnp.where((row == 0) | (row == 6), edge, matrix_edge_ref[...])


def lat_matrix(kappa_lat, sea_mask, kappa_lon):
    shape = kappa_lat.shape
    steps = (shape[1] - 1).bit_length()
    full = jax.ShapeDtypeStruct(shape, jnp.float32)
    stacked = jax.ShapeDtypeStruct((steps,) + shape, jnp.float32)
    edge = jax.ShapeDtypeStruct((shape[0], 8, shape[2]), jnp.float32)
    return pl.pallas_call(
        lat_matrix_kernel,
        out_shape=(full, full, stacked, stacked, full, edge, full),
    )(kappa_lat, sea_mask, kappa_lon)


def lat_rhs(*inputs):
    shape = inputs[0].shape
    return pl.pallas_call(
        lat_rhs_kernel,
        out_shape=(
            jax.ShapeDtypeStruct(shape, jnp.float32),
            jax.ShapeDtypeStruct((shape[0], 8, shape[2]), jnp.float32),
        ),
    )(*inputs)


def circular_solve(lower_band, upper_band, excess, sources):
    devices = lower_band.shape[0]
    stride = 1
    while stride < devices:
        inverse = 1.0 / (excess - lower_band - upper_band)
        left_weight = -lower_band * jnp.roll(inverse, stride, 0)
        right_coefficient = -upper_band * jnp.roll(inverse, -stride, 0)
        new_lower = left_weight * jnp.roll(lower_band, stride, 0)
        new_upper = right_coefficient * jnp.roll(upper_band, -stride, 0)
        excess = (
            excess
            + left_weight * jnp.roll(excess, stride, 0)
            + right_coefficient * jnp.roll(excess, -stride, 0)
        )
        sources = (
            sources
            + left_weight * jnp.roll(sources, stride, 0)
            + right_coefficient * jnp.roll(sources, -stride, 0)
        )
        lower_band, upper_band = (new_lower, new_upper)
        stride = stride * 2
    return sources / excess


def interface_flux(edge, axis, mesh_axis, periodic, exchange):
    terms = lax.slice_in_dim(edge, 0, TERMS, axis=axis)
    devices = lax.axis_size(mesh_axis)
    if exchange == "all_to_all":
        copies = jnp.broadcast_to(terms[None], (devices,) + terms.shape)
        gathered = lax.all_to_all(copies, mesh_axis, 0, 0, tiled=True)
    else:
        gathered = lax.all_gather(terms[None], mesh_axis, axis=0, tiled=True)
    (head_p, head_u, head_w, tail_kappa, tail_u, tail_w, tail_p) = (
        lax.index_in_dim(gathered, k, axis + 1, keepdims=False) for k in range(TERMS)
    )

    def next_of(member):
        return jnp.roll(member, -1, 0)

    next_wet = jnp.where(next_of(head_u) > 0.0, 1.0, 0.0)
    face = tail_kappa * next_wet
    if not periodic:
        device = lax.broadcasted_iota(jnp.int32, face.shape, 0)
        face = jnp.where(device == devices - 1, 0.0, face)
        tail_kappa = jnp.where(device == devices - 1, 0.0, tail_kappa)
    lower = -face * tail_u
    upper = -tail_kappa * next_of(head_w)
    diagonal = 1.0 + tail_kappa * next_of(head_u) + face * tail_w
    flux = circular_solve(
        lower, upper, diagonal + lower + upper, tail_kappa * next_of(head_p) - face * tail_p
    )
    index = lax.axis_index(mesh_axis)
    here = lax.dynamic_index_in_dim(flux, index, 0, keepdims=True)
    before = lax.dynamic_index_in_dim(flux, (index + devices - 1) % devices, 0, keepdims=True)
    return before[0], here[0]


def shards(source, kappa_lon, kappa_lat, sea_mask):
    p_lon, u_lon, w_lon, edge_lon = local_pass(2, (source, kappa_lon, sea_mask))
    u_lat, w_lat, left, right, diagonal, matrix_edge, scale = lat_matrix(kappa_lat, sea_mask, kappa_lon)
    before, here = interface_flux(edge_lon, 2, "lon", True, "all_to_all")
    p_lat, edge_lat = lat_rhs(
        p_lon, u_lon, w_lon, before[:, :, None], here[:, :, None], sea_mask,
        left, right, diagonal, matrix_edge,
    )
    before, here = interface_flux(edge_lat, 1, "lat", False, "all_gather")
    return scale * (p_lat - u_lat * before[:, None, :] + w_lat * here[:, None, :])


def solution(mesh):
    return jax.shard_map(
        shards,
        mesh=mesh,
        in_specs=(
            P(None, "lat", "lon"),
            P(None, "lat", "lon"),
            P(None, "lat", "lon"),
            P(None, "lat", "lon"),
        ),
        out_specs=P(None, "lat", "lon"),
        check_vma=False,
    )
```

```python
import functools

import jax
import jax.numpy as jnp
from jax import lax
from jax.experimental import pallas as pl
from jax.experimental.pallas import tpu as pltpu
from jax.sharding import PartitionSpec as P

TERMS = 7


def shifted(values, shift, axis):
    length = values.shape[axis]
    return pltpu.roll(values, shift % length, axis)


def block_solve(lower_band, upper_band, excess, sources, axis, weights=None):
    length = lower_band.shape[axis]
    stride = 1
    while stride < length:
        inverse = 1.0 / (excess - lower_band - upper_band)
        left_weight = -lower_band * shifted(inverse, stride, axis)
        right_coefficient = -upper_band * shifted(inverse, -stride, axis)
        if weights is not None:
            weights.append((left_weight, right_coefficient))
        new_lower = left_weight * shifted(lower_band, stride, axis)
        new_upper = right_coefficient * shifted(upper_band, -stride, axis)
        excess = (
            excess
            + left_weight * shifted(excess, stride, axis)
            + right_coefficient * shifted(excess, -stride, axis)
        )
        sources = [
            member
            + left_weight * shifted(member, stride, axis)
            + right_coefficient * shifted(member, -stride, axis)
            for member in sources
        ]
        lower_band, upper_band = (new_lower, new_upper)
        stride = stride * 2
    diagonal = excess - lower_band - upper_band
    if weights is not None:
        weights.append(diagonal)
    return [member / diagonal for member in sources]


def pass_kernel(axis, corrected, *refs):
    if corrected:
        (p_ref, u_ref, w_ref, before_ref, here_ref, kappa_ref, mask_ref,
         p_out, u_out, w_out, edge_out) = refs
        values = (
            p_ref[...]
            - u_ref[...] * before_ref[...]
            + w_ref[...] * here_ref[...]
        )
    else:
        (source_ref, kappa_ref, mask_ref, p_out, u_out, w_out, edge_out) = refs
        values = source_ref[...]
    shape = values.shape
    length = shape[axis]
    wet = mask_ref[...].astype(jnp.float32)
    weight = kappa_ref[...].astype(jnp.float32) * wet
    position = lax.broadcasted_iota(jnp.int32, shape, axis)
    last = position == length - 1
    right_face = jnp.where(last, 0.0, weight * shifted(wet, -1, axis))
    left_face = shifted(right_face, 1, axis)
    first = position == 0
    particular, from_left, from_right = block_solve(
        -left_face,
        -right_face,
        jnp.ones(shape, jnp.float32),
        [values, jnp.where(first, 1.0, 0.0), jnp.where(last, 1.0, 0.0)],
        axis,
    )
    p_out[...] = particular
    u_out[...] = from_left
    w_out[...] = from_right
    tail_weight = shifted(weight, 4, axis)
    entries = [
        wet * particular,
        shifted(wet * from_left, 1, axis),
        shifted(wet * from_right, 2, axis),
        tail_weight,
        shifted(from_left, 4 + 1, axis),
        shifted(from_right, 4 + 2, axis),
        shifted(particular, 4 + 3, axis),
    ]
    edge = entries[0]
    for k in range(1, TERMS):
        edge = jnp.where(position == k, entries[k], edge)
    if axis == 2:
        edge_out[...] = edge
    else:
        edge_out[...] = lax.slice_in_dim(edge, 0, 8, axis=axis)


def local_pass(axis, inputs):
    shape = inputs[0].shape
    corrected = len(inputs) > 3
    edge_shape = shape if axis == 2 else shape[:axis] + (8,) + shape[axis + 1:]
    return pl.pallas_call(
        functools.partial(pass_kernel, axis, corrected),
        out_shape=(
            jax.ShapeDtypeStruct(shape, jnp.float32),
            jax.ShapeDtypeStruct(shape, jnp.float32),
            jax.ShapeDtypeStruct(shape, jnp.float32),
            jax.ShapeDtypeStruct(edge_shape, jnp.float32),
        ),
    )(*inputs)


def lat_matrix_kernel(kappa_ref, mask_ref, lon_kappa_ref, u_out, w_out, left_out, right_out,
                      diagonal_out, edge_out, scale_out, weight_scratch):
    axis = 1
    wet = mask_ref[...].astype(jnp.float32)
    lat_kappa = kappa_ref[...].astype(jnp.float32)
    scale_out[...] = wet * 4.0 * jnp.sqrt(jnp.sqrt(lon_kappa_ref[...].astype(jnp.float32) * lat_kappa))
    weight = lat_kappa * wet
    shape = wet.shape
    length = shape[axis]
    position = lax.broadcasted_iota(jnp.int32, shape, axis)
    last = position == length - 1
    right_face = jnp.where(last, 0.0, weight * shifted(wet, -1, axis))
    left_face = shifted(right_face, 1, axis)
    weights = []
    from_left, from_right = block_solve(
        -left_face,
        -right_face,
        jnp.ones(shape, jnp.float32),
        [jnp.where(position == 0, 1.0, 0.0), jnp.where(last, 1.0, 0.0)],
        axis,
        weights,
    )
    u_out[...] = from_left
    w_out[...] = from_right
    for step, (left_weight, right_coefficient) in enumerate(weights[:-1]):
        left_out[step] = left_weight
        right_out[step] = right_coefficient
    diagonal_out[...] = weights[-1]
    weight_scratch[...] = weight
    head_wet = mask_ref[:, 0, :].astype(jnp.float32)
    edge_out[0] = head_wet * u_out[:, 0, :]
    edge_out[1] = head_wet * w_out[:, 0, :]
    edge_out[2] = weight_scratch[:, length - 1, :]
    edge_out[3] = u_out[:, length - 1, :]
    edge_out[4] = w_out[:, length - 1, :]


def lat_rhs_kernel(p_ref, u_ref, w_ref, flux_ref, mask_ref, left_ref, right_ref,
                   diagonal_ref, matrix_edge_ref, p_out, edge_out):
    axis = 1
    values = p_ref[...] - u_ref[...] * flux_ref[0] + w_ref[...] * flux_ref[1]
    length = values.shape[axis]
    stride = 1
    step = 0
    while stride < length:
        values = (
            values
            + left_ref[step] * shifted(values, stride, axis)
            + right_ref[step] * shifted(values, -stride, axis)
        )
        stride = stride * 2
        step = step + 1
    p_out[...] = values / diagonal_ref[...]
    edge_out[0] = mask_ref[:, 0, :].astype(jnp.float32) * p_out[:, 0, :]
    edge_out[1:TERMS - 1] = matrix_edge_ref[...]
    edge_out[TERMS - 1] = p_out[:, length - 1, :]


def lat_matrix(kappa_lat, sea_mask, kappa_lon):
    shape = kappa_lat.shape
    steps = (shape[1] - 1).bit_length()
    full = jax.ShapeDtypeStruct(shape, jnp.float32)
    stacked = jax.ShapeDtypeStruct((steps,) + shape, jnp.float32)
    edge = jax.ShapeDtypeStruct((TERMS - 2, shape[0], shape[2]), jnp.float32)
    return pl.pallas_call(
        lat_matrix_kernel,
        out_shape=(full, full, stacked, stacked, full, edge, full),
        scratch_shapes=[pltpu.VMEM(shape, jnp.float32)],
    )(kappa_lat, sea_mask, kappa_lon)


def lat_rhs(*inputs):
    shape = inputs[0].shape
    return pl.pallas_call(
        lat_rhs_kernel,
        out_shape=(
            jax.ShapeDtypeStruct(shape, jnp.float32),
            jax.ShapeDtypeStruct((TERMS, shape[0], shape[2]), jnp.float32),
        ),
    )(*inputs)


def circular_solve(lower_band, upper_band, excess, sources):
    devices = lower_band.shape[0]
    stride = 1
    while stride < devices:
        inverse = 1.0 / (excess - lower_band - upper_band)
        left_weight = -lower_band * jnp.roll(inverse, stride, 0)
        right_coefficient = -upper_band * jnp.roll(inverse, -stride, 0)
        new_lower = left_weight * jnp.roll(lower_band, stride, 0)
        new_upper = right_coefficient * jnp.roll(upper_band, -stride, 0)
        excess = (
            excess
            + left_weight * jnp.roll(excess, stride, 0)
            + right_coefficient * jnp.roll(excess, -stride, 0)
        )
        sources = (
            sources
            + left_weight * jnp.roll(sources, stride, 0)
            + right_coefficient * jnp.roll(sources, -stride, 0)
        )
        lower_band, upper_band = (new_lower, new_upper)
        stride = stride * 2
    return sources / excess


def interface_flux(edge, axis, mesh_axis, periodic, exchange):
    terms = lax.slice_in_dim(edge, 0, TERMS, axis=axis) if edge.shape[axis] > TERMS else edge
    devices = lax.axis_size(mesh_axis)
    if exchange == "all_to_all":
        copies = jnp.broadcast_to(terms[None], (devices,) + terms.shape)
        gathered = lax.all_to_all(copies, mesh_axis, 0, 0, tiled=True)
    else:
        gathered = lax.all_gather(terms[None], mesh_axis, axis=0, tiled=True)
    (head_p, head_u, head_w, tail_kappa, tail_u, tail_w, tail_p) = (
        lax.index_in_dim(gathered, k, axis + 1, keepdims=False) for k in range(TERMS)
    )

    def next_of(member):
        return jnp.roll(member, -1, 0)

    next_wet = jnp.where(next_of(head_u) > 0.0, 1.0, 0.0)
    face = tail_kappa * next_wet
    if not periodic:
        device = lax.broadcasted_iota(jnp.int32, face.shape, 0)
        face = jnp.where(device == devices - 1, 0.0, face)
        tail_kappa = jnp.where(device == devices - 1, 0.0, tail_kappa)
    lower = -face * tail_u
    upper = -tail_kappa * next_of(head_w)
    diagonal = 1.0 + tail_kappa * next_of(head_u) + face * tail_w
    flux = circular_solve(
        lower, upper, diagonal + lower + upper, tail_kappa * next_of(head_p) - face * tail_p
    )
    index = lax.axis_index(mesh_axis)
    here = lax.dynamic_index_in_dim(flux, index, 0, keepdims=True)
    before = lax.dynamic_index_in_dim(flux, (index + devices - 1) % devices, 0, keepdims=True)
    return before[0], here[0]


def shards(source, kappa_lon, kappa_lat, sea_mask):
    p_lon, u_lon, w_lon, edge_lon = local_pass(2, (source, kappa_lon, sea_mask))
    u_lat, w_lat, left, right, diagonal, matrix_edge, scale = lat_matrix(kappa_lat, sea_mask, kappa_lon)
    before, here = interface_flux(edge_lon, 2, "lon", True, "all_to_all")
    p_lat, edge_lat = lat_rhs(
        p_lon, u_lon, w_lon, jnp.stack([before, here], 0)[..., None], sea_mask,
        left, right, diagonal, matrix_edge,
    )
    before, here = interface_flux(edge_lat, 0, "lat", False, "all_gather")
    return scale * (p_lat - u_lat * before[:, None, :] + w_lat * here[:, None, :])


def solution(mesh):
    return jax.shard_map(
        shards,
        mesh=mesh,
        in_specs=(
            P(None, "lat", "lon"),
            P(None, "lat", "lon"),
            P(None, "lat", "lon"),
            P(None, "lat", "lon"),
        ),
        out_specs=P(None, "lat", "lon"),
        check_vma=False,
    )
```

```python
import functools

import jax
import jax.numpy as jnp
from jax import lax
from jax.experimental import pallas as pl
from jax.experimental.pallas import tpu as pltpu
from jax.sharding import PartitionSpec as P

TERMS = 7


def shifted(values, shift, axis):
    length = values.shape[axis]
    return pltpu.roll(values, shift % length, axis)


def block_solve(lower_band, upper_band, excess, sources, axis, weights=None):
    length = lower_band.shape[axis]
    stride = 1
    while stride < length:
        inverse = 1.0 / (excess - lower_band - upper_band)
        left_weight = -lower_band * shifted(inverse, stride, axis)
        right_coefficient = -upper_band * shifted(inverse, -stride, axis)
        if weights is not None:
            weights.append((left_weight, right_coefficient))
        new_lower = left_weight * shifted(lower_band, stride, axis)
        new_upper = right_coefficient * shifted(upper_band, -stride, axis)
        excess = (
            excess
            + left_weight * shifted(excess, stride, axis)
            + right_coefficient * shifted(excess, -stride, axis)
        )
        sources = [
            member
            + left_weight * shifted(member, stride, axis)
            + right_coefficient * shifted(member, -stride, axis)
            for member in sources
        ]
        lower_band, upper_band = (new_lower, new_upper)
        stride = stride * 2
    diagonal = excess - lower_band - upper_band
    if weights is not None:
        weights.append(diagonal)
    return [member / diagonal for member in sources]


def pass_kernel(axis, corrected, *refs):
    if corrected:
        (p_ref, u_ref, w_ref, before_ref, here_ref, kappa_ref, mask_ref,
         p_out, u_out, w_out, edge_out) = refs
        values = (
            p_ref[...]
            - u_ref[...] * before_ref[...]
            + w_ref[...] * here_ref[...]
        )
    else:
        (source_ref, kappa_ref, mask_ref, p_out, u_out, w_out, edge_out) = refs
        values = source_ref[...]
    shape = values.shape
    length = shape[axis]
    wet = mask_ref[...].astype(jnp.float32)
    weight = kappa_ref[...].astype(jnp.float32) * wet
    position = lax.broadcasted_iota(jnp.int32, shape, axis)
    last = position == length - 1
    right_face = jnp.where(last, 0.0, weight * shifted(wet, -1, axis))
    left_face = shifted(right_face, 1, axis)
    first = position == 0
    particular, from_left, from_right = block_solve(
        -left_face,
        -right_face,
        jnp.ones(shape, jnp.float32),
        [values, jnp.where(first, 1.0, 0.0), jnp.where(last, 1.0, 0.0)],
        axis,
    )
    p_out[...] = particular
    u_out[...] = from_left
    w_out[...] = from_right
    tail_weight = shifted(weight, 4, axis)
    entries = [
        wet * particular,
        shifted(wet * from_left, 1, axis),
        shifted(wet * from_right, 2, axis),
        tail_weight,
        shifted(from_left, 4 + 1, axis),
        shifted(from_right, 4 + 2, axis),
        shifted(particular, 4 + 3, axis),
    ]
    edge = entries[0]
    for k in range(1, TERMS):
        edge = jnp.where(position == k, entries[k], edge)
    if axis == 2:
        edge_out[...] = edge
    else:
        edge_out[...] = lax.slice_in_dim(edge, 0, 8, axis=axis)


def local_pass(axis, inputs):
    shape = inputs[0].shape
    corrected = len(inputs) > 3
    edge_shape = shape if axis == 2 else shape[:axis] + (8,) + shape[axis + 1:]
    return pl.pallas_call(
        functools.partial(pass_kernel, axis, corrected),
        out_shape=(
            jax.ShapeDtypeStruct(shape, jnp.float32),
            jax.ShapeDtypeStruct(shape, jnp.float32),
            jax.ShapeDtypeStruct(shape, jnp.float32),
            jax.ShapeDtypeStruct(edge_shape, jnp.float32),
        ),
    )(*inputs)


def lat_matrix_kernel(kappa_ref, mask_ref, lon_kappa_ref, u_out, w_out, left_out, right_out,
                      diagonal_out, edge_out, scale_out, weight_scratch):
    axis = 1
    wet = mask_ref[...].astype(jnp.float32)
    lat_kappa = kappa_ref[...].astype(jnp.float32)
    scale_out[...] = wet * 4.0 * jnp.sqrt(jnp.sqrt(lon_kappa_ref[...].astype(jnp.float32) * lat_kappa))
    weight = lat_kappa * wet
    shape = wet.shape
    length = shape[axis]
    position = lax.broadcasted_iota(jnp.int32, shape, axis)
    last = position == length - 1
    right_face = jnp.where(last, 0.0, weight * shifted(wet, -1, axis))
    left_face = shifted(right_face, 1, axis)
    weights = []
    from_left, from_right = block_solve(
        -left_face,
        -right_face,
        jnp.ones(shape, jnp.float32),
        [jnp.where(position == 0, 1.0, 0.0), jnp.where(last, 1.0, 0.0)],
        axis,
        weights,
    )
    u_out[...] = from_left
    w_out[...] = from_right
    for step, (left_weight, right_coefficient) in enumerate(weights[:-1]):
        left_out[step] = left_weight
        right_out[step] = right_coefficient
    diagonal_out[...] = weights[-1]
    weight_scratch[...] = weight
    head_wet = mask_ref[:, 0, :].astype(jnp.float32)
    edge_out[0] = head_wet * u_out[:, 0, :]
    edge_out[1] = head_wet * w_out[:, 0, :]
    edge_out[2] = weight_scratch[:, length - 1, :]
    edge_out[3] = u_out[:, length - 1, :]
    edge_out[4] = w_out[:, length - 1, :]


def lat_rhs_kernel(p_ref, u_ref, w_ref, flux_ref, mask_ref, left_ref, right_ref,
                   diagonal_ref, matrix_edge_ref, p_out, edge_out):
    axis = 1
    values = p_ref[...] - u_ref[...] * flux_ref[0] + w_ref[...] * flux_ref[1]
    length = values.shape[axis]
    stride = 1
    step = 0
    while stride < length:
        values = (
            values
            + left_ref[step] * shifted(values, stride, axis)
            + right_ref[step] * shifted(values, -stride, axis)
        )
        stride = stride * 2
        step = step + 1
    p_out[...] = values / diagonal_ref[...]
    edge_out[0] = mask_ref[:, 0, :].astype(jnp.float32) * p_out[:, 0, :]
    edge_out[1:TERMS - 1] = matrix_edge_ref[...]
    edge_out[TERMS - 1] = p_out[:, length - 1, :]


def lat_matrix(kappa_lat, sea_mask, kappa_lon):
    shape = kappa_lat.shape
    steps = (shape[1] - 1).bit_length()
    full = jax.ShapeDtypeStruct(shape, jnp.float32)
    stacked = jax.ShapeDtypeStruct((steps,) + shape, jnp.float32)
    edge = jax.ShapeDtypeStruct((TERMS - 2, shape[0], shape[2]), jnp.float32)
    return pl.pallas_call(
        lat_matrix_kernel,
        out_shape=(full, full, stacked, stacked, full, edge, full),
        scratch_shapes=[pltpu.VMEM(shape, jnp.float32)],
    )(kappa_lat, sea_mask, kappa_lon)


def lat_rhs(*inputs):
    shape = inputs[0].shape
    return pl.pallas_call(
        lat_rhs_kernel,
        out_shape=(
            jax.ShapeDtypeStruct(shape, jnp.float32),
            jax.ShapeDtypeStruct((TERMS, shape[0], shape[2]), jnp.float32),
        ),
    )(*inputs)


def circular_solve(lower_band, upper_band, excess, sources, roll=jnp.roll):
    devices = lower_band.shape[0]
    stride = 1
    while stride < devices:
        inverse = 1.0 / (excess - lower_band - upper_band)
        left_weight = -lower_band * roll(inverse, stride, 0)
        right_coefficient = -upper_band * roll(inverse, -stride, 0)
        new_lower = left_weight * roll(lower_band, stride, 0)
        new_upper = right_coefficient * roll(upper_band, -stride, 0)
        excess = (
            excess
            + left_weight * roll(excess, stride, 0)
            + right_coefficient * roll(excess, -stride, 0)
        )
        sources = (
            sources
            + left_weight * roll(sources, stride, 0)
            + right_coefficient * roll(sources, -stride, 0)
        )
        lower_band, upper_band = (new_lower, new_upper)
        stride = stride * 2
    return sources / excess


def leading_roll(values, shift, axis):
    shift = shift % values.shape[axis]
    if shift == 0:
        return values
    length = values.shape[axis]
    return jnp.concatenate(
        [
            lax.slice_in_dim(values, length - shift, length, axis=axis),
            lax.slice_in_dim(values, 0, length - shift, axis=axis),
        ],
        axis,
    )


def flux_system(terms, periodic, roll):
    head_p, head_u, head_w, tail_kappa, tail_u, tail_w, tail_p = terms
    devices = head_p.shape[0]

    def next_of(member):
        return roll(member, -1, 0)

    next_wet = jnp.where(next_of(head_u) > 0.0, 1.0, 0.0)
    face = tail_kappa * next_wet
    if not periodic:
        device = lax.broadcasted_iota(jnp.int32, face.shape, 0)
        face = jnp.where(device == devices - 1, 0.0, face)
        tail_kappa = jnp.where(device == devices - 1, 0.0, tail_kappa)
    lower = -face * tail_u
    upper = -tail_kappa * next_of(head_w)
    diagonal = 1.0 + tail_kappa * next_of(head_u) + face * tail_w
    return circular_solve(
        lower, upper, diagonal + lower + upper, tail_kappa * next_of(head_p) - face * tail_p, roll
    )


def final_kernel(index_ref, gathered_ref, scale_ref, p_ref, u_ref, w_ref, out_ref, flux_scratch):
    terms = [gathered_ref[:, k] for k in range(TERMS)]
    flux_scratch[...] = flux_system(terms, False, leading_roll)
    devices = flux_scratch.shape[0]
    index = index_ref[0]
    here = flux_scratch[index]
    before = flux_scratch[(index + devices - 1) % devices]
    out_ref[...] = scale_ref[...] * (
        p_ref[...] - u_ref[...] * before[:, None, :] + w_ref[...] * here[:, None, :]
    )


def lat_final(edge, scale, p_lat, u_lat, w_lat):
    gathered = lax.all_gather(edge[None], "lat", axis=0, tiled=True)
    index = jnp.full((1,), lax.axis_index("lat"), jnp.int32)
    vmem = pl.BlockSpec(memory_space=pltpu.VMEM)
    return pl.pallas_call(
        final_kernel,
        out_shape=jax.ShapeDtypeStruct(p_lat.shape, jnp.float32),
        in_specs=[pl.BlockSpec(memory_space=pltpu.SMEM)] + [vmem] * 5,
        out_specs=vmem,
        scratch_shapes=[pltpu.VMEM((gathered.shape[0],) + edge.shape[1:], jnp.float32)],
    )(index, gathered, scale, p_lat, u_lat, w_lat)


def interface_flux(edge, axis, mesh_axis, periodic, exchange):
    terms = lax.slice_in_dim(edge, 0, TERMS, axis=axis) if edge.shape[axis] > TERMS else edge
    devices = lax.axis_size(mesh_axis)
    if exchange == "all_to_all":
        copies = jnp.broadcast_to(terms[None], (devices,) + terms.shape)
        gathered = lax.all_to_all(copies, mesh_axis, 0, 0, tiled=True)
    else:
        gathered = lax.all_gather(terms[None], mesh_axis, axis=0, tiled=True)
    terms = [lax.index_in_dim(gathered, k, axis + 1, keepdims=False) for k in range(TERMS)]
    flux = flux_system(terms, periodic, jnp.roll)
    index = lax.axis_index(mesh_axis)
    here = lax.dynamic_index_in_dim(flux, index, 0, keepdims=True)
    before = lax.dynamic_index_in_dim(flux, (index + devices - 1) % devices, 0, keepdims=True)
    return before[0], here[0]


def shards(source, kappa_lon, kappa_lat, sea_mask):
    p_lon, u_lon, w_lon, edge_lon = local_pass(2, (source, kappa_lon, sea_mask))
    u_lat, w_lat, left, right, diagonal, matrix_edge, scale = lat_matrix(kappa_lat, sea_mask, kappa_lon)
    before, here = interface_flux(edge_lon, 2, "lon", True, "all_to_all")
    p_lat, edge_lat = lat_rhs(
        p_lon, u_lon, w_lon, jnp.stack([before, here], 0)[..., None], sea_mask,
        left, right, diagonal, matrix_edge,
    )
    return lat_final(edge_lat, scale, p_lat, u_lat, w_lat)


def solution(mesh):
    return jax.shard_map(
        shards,
        mesh=mesh,
        in_specs=(
            P(None, "lat", "lon"),
            P(None, "lat", "lon"),
            P(None, "lat", "lon"),
            P(None, "lat", "lon"),
        ),
        out_specs=P(None, "lat", "lon"),
        check_vma=False,
    )
```

```python
import functools

import jax
import jax.numpy as jnp
from jax import lax
from jax.experimental import pallas as pl
from jax.experimental.pallas import tpu as pltpu
from jax.sharding import PartitionSpec as P

TERMS = 7


def shifted(values, shift, axis):
    length = values.shape[axis]
    return pltpu.roll(values, shift % length, axis)


def block_solve(lower_band, upper_band, excess, sources, axis, weights=None):
    length = lower_band.shape[axis]
    stride = 1
    while stride < length:
        inverse = 1.0 / (excess - lower_band - upper_band)
        left_weight = -lower_band * shifted(inverse, stride, axis)
        right_coefficient = -upper_band * shifted(inverse, -stride, axis)
        if weights is not None:
            weights.append((left_weight, right_coefficient))
        new_lower = left_weight * shifted(lower_band, stride, axis)
        new_upper = right_coefficient * shifted(upper_band, -stride, axis)
        excess = (
            excess
            + left_weight * shifted(excess, stride, axis)
            + right_coefficient * shifted(excess, -stride, axis)
        )
        sources = [
            member
            + left_weight * shifted(member, stride, axis)
            + right_coefficient * shifted(member, -stride, axis)
            for member in sources
        ]
        lower_band, upper_band = (new_lower, new_upper)
        stride = stride * 2
    diagonal = excess - lower_band - upper_band
    if weights is not None:
        weights.append(diagonal)
    return [member / diagonal for member in sources]


def pass_kernel(axis, corrected, *refs):
    if corrected:
        (p_ref, u_ref, w_ref, before_ref, here_ref, kappa_ref, mask_ref,
         p_out, u_out, w_out, edge_out) = refs
        values = (
            p_ref[...]
            - u_ref[...] * before_ref[...]
            + w_ref[...] * here_ref[...]
        )
    else:
        (source_ref, kappa_ref, mask_ref, p_out, u_out, w_out, edge_out) = refs
        values = source_ref[...]
    shape = values.shape
    length = shape[axis]
    wet = mask_ref[...].astype(jnp.float32)
    weight = kappa_ref[...].astype(jnp.float32) * wet
    position = lax.broadcasted_iota(jnp.int32, shape, axis)
    last = position == length - 1
    right_face = jnp.where(last, 0.0, weight * shifted(wet, -1, axis))
    left_face = shifted(right_face, 1, axis)
    first = position == 0
    particular, from_left, from_right = block_solve(
        -left_face,
        -right_face,
        jnp.ones(shape, jnp.float32),
        [values, jnp.where(first, 1.0, 0.0), jnp.where(last, 1.0, 0.0)],
        axis,
    )
    p_out[...] = particular
    u_out[...] = from_left
    w_out[...] = from_right
    tail_weight = shifted(weight, 4, axis)
    entries = [
        wet * particular,
        shifted(wet * from_left, 1, axis),
        shifted(wet * from_right, 2, axis),
        tail_weight,
        shifted(from_left, 4 + 1, axis),
        shifted(from_right, 4 + 2, axis),
        shifted(particular, 4 + 3, axis),
    ]
    edge = entries[0]
    for k in range(1, TERMS):
        edge = jnp.where(position == k, entries[k], edge)
    if axis == 2:
        edge_out[...] = edge
    else:
        edge_out[...] = lax.slice_in_dim(edge, 0, 8, axis=axis)


def local_pass(axis, inputs):
    shape = inputs[0].shape
    corrected = len(inputs) > 3
    edge_shape = shape if axis == 2 else shape[:axis] + (8,) + shape[axis + 1:]
    return pl.pallas_call(
        functools.partial(pass_kernel, axis, corrected),
        out_shape=(
            jax.ShapeDtypeStruct(shape, jnp.float32),
            jax.ShapeDtypeStruct(shape, jnp.float32),
            jax.ShapeDtypeStruct(shape, jnp.float32),
            jax.ShapeDtypeStruct(edge_shape, jnp.float32),
        ),
    )(*inputs)


def lon_kernel(source_ref, kappa_ref, mask_ref, p_out, u_out, w_out, edge_out):
    levels, rows, length = source_ref.shape
    lines = levels * rows

    def across(values):
        return jnp.transpose(values.astype(jnp.float32).reshape(lines, length))

    def back(values):
        return jnp.transpose(values).reshape(levels, rows, length)

    wet = across(mask_ref[...])
    weight = across(kappa_ref[...]) * wet
    values = across(source_ref[...])
    axis = 0
    shape = values.shape
    position = lax.broadcasted_iota(jnp.int32, shape, axis)
    last = position == length - 1
    right_face = jnp.where(last, 0.0, weight * shifted(wet, -1, axis))
    left_face = shifted(right_face, 1, axis)
    particular, from_left, from_right = block_solve(
        -left_face,
        -right_face,
        jnp.ones(shape, jnp.float32),
        [values, jnp.where(position == 0, 1.0, 0.0), jnp.where(last, 1.0, 0.0)],
        axis,
    )
    p_out[...] = back(particular)
    u_out[...] = back(from_left)
    w_out[...] = back(from_right)
    head_wet = wet[0:1, :]
    edge_out[0:1, :] = head_wet * particular[0:1, :]
    edge_out[1:2, :] = head_wet * from_left[0:1, :]
    edge_out[2:3, :] = head_wet * from_right[0:1, :]
    edge_out[3:4, :] = weight[length - 1:length, :]
    edge_out[4:5, :] = from_left[length - 1:length, :]
    edge_out[5:6, :] = from_right[length - 1:length, :]
    edge_out[6:7, :] = particular[length - 1:length, :]


def lon_pass(source, kappa_lon, sea_mask):
    shape = source.shape
    full = jax.ShapeDtypeStruct(shape, jnp.float32)
    return pl.pallas_call(
        lon_kernel,
        out_shape=(full, full, full, jax.ShapeDtypeStruct((TERMS, shape[0] * shape[1]), jnp.float32)),
    )(source, kappa_lon, sea_mask)


def lat_matrix_kernel(kappa_ref, mask_ref, lon_kappa_ref, u_out, w_out, left_out, right_out,
                      diagonal_out, edge_out, scale_out, weight_scratch):
    axis = 1
    wet = mask_ref[...].astype(jnp.float32)
    lat_kappa = kappa_ref[...].astype(jnp.float32)
    scale_out[...] = wet * 4.0 * jnp.sqrt(jnp.sqrt(lon_kappa_ref[...].astype(jnp.float32) * lat_kappa))
    weight = lat_kappa * wet
    shape = wet.shape
    length = shape[axis]
    position = lax.broadcasted_iota(jnp.int32, shape, axis)
    last = position == length - 1
    right_face = jnp.where(last, 0.0, weight * shifted(wet, -1, axis))
    left_face = shifted(right_face, 1, axis)
    weights = []
    from_left, from_right = block_solve(
        -left_face,
        -right_face,
        jnp.ones(shape, jnp.float32),
        [jnp.where(position == 0, 1.0, 0.0), jnp.where(last, 1.0, 0.0)],
        axis,
        weights,
    )
    u_out[...] = from_left
    w_out[...] = from_right
    for step, (left_weight, right_coefficient) in enumerate(weights[:-1]):
        left_out[step] = left_weight
        right_out[step] = right_coefficient
    diagonal_out[...] = weights[-1]
    weight_scratch[...] = weight
    head_wet = mask_ref[:, 0, :].astype(jnp.float32)
    edge_out[0] = head_wet * u_out[:, 0, :]
    edge_out[1] = head_wet * w_out[:, 0, :]
    edge_out[2] = weight_scratch[:, length - 1, :]
    edge_out[3] = u_out[:, length - 1, :]
    edge_out[4] = w_out[:, length - 1, :]


def lat_rhs_kernel(p_ref, u_ref, w_ref, flux_ref, mask_ref, left_ref, right_ref,
                   diagonal_ref, matrix_edge_ref, p_out, edge_out):
    axis = 1
    values = p_ref[...] - u_ref[...] * flux_ref[0] + w_ref[...] * flux_ref[1]
    length = values.shape[axis]
    stride = 1
    step = 0
    while stride < length:
        values = (
            values
            + left_ref[step] * shifted(values, stride, axis)
            + right_ref[step] * shifted(values, -stride, axis)
        )
        stride = stride * 2
        step = step + 1
    p_out[...] = values / diagonal_ref[...]
    edge_out[0] = mask_ref[:, 0, :].astype(jnp.float32) * p_out[:, 0, :]
    edge_out[1:TERMS - 1] = matrix_edge_ref[...]
    edge_out[TERMS - 1] = p_out[:, length - 1, :]


def lat_matrix(kappa_lat, sea_mask, kappa_lon):
    shape = kappa_lat.shape
    steps = (shape[1] - 1).bit_length()
    full = jax.ShapeDtypeStruct(shape, jnp.float32)
    stacked = jax.ShapeDtypeStruct((steps,) + shape, jnp.float32)
    edge = jax.ShapeDtypeStruct((TERMS - 2, shape[0], shape[2]), jnp.float32)
    return pl.pallas_call(
        lat_matrix_kernel,
        out_shape=(full, full, stacked, stacked, full, edge, full),
        scratch_shapes=[pltpu.VMEM(shape, jnp.float32)],
    )(kappa_lat, sea_mask, kappa_lon)


def lat_rhs(*inputs):
    shape = inputs[0].shape
    return pl.pallas_call(
        lat_rhs_kernel,
        out_shape=(
            jax.ShapeDtypeStruct(shape, jnp.float32),
            jax.ShapeDtypeStruct((TERMS, shape[0], shape[2]), jnp.float32),
        ),
    )(*inputs)


def circular_solve(lower_band, upper_band, excess, sources):
    devices = lower_band.shape[0]
    stride = 1
    while stride < devices:
        inverse = 1.0 / (excess - lower_band - upper_band)
        left_weight = -lower_band * jnp.roll(inverse, stride, 0)
        right_coefficient = -upper_band * jnp.roll(inverse, -stride, 0)
        new_lower = left_weight * jnp.roll(lower_band, stride, 0)
        new_upper = right_coefficient * jnp.roll(upper_band, -stride, 0)
        excess = (
            excess
            + left_weight * jnp.roll(excess, stride, 0)
            + right_coefficient * jnp.roll(excess, -stride, 0)
        )
        sources = (
            sources
            + left_weight * jnp.roll(sources, stride, 0)
            + right_coefficient * jnp.roll(sources, -stride, 0)
        )
        lower_band, upper_band = (new_lower, new_upper)
        stride = stride * 2
    return sources / excess


def flux_system(terms, periodic):
    head_p, head_u, head_w, tail_kappa, tail_u, tail_w, tail_p = terms
    devices = head_p.shape[0]

    def next_of(member):
        return jnp.roll(member, -1, 0)

    next_wet = jnp.where(next_of(head_u) > 0.0, 1.0, 0.0)
    face = tail_kappa * next_wet
    if not periodic:
        device = lax.broadcasted_iota(jnp.int32, face.shape, 0)
        face = jnp.where(device == devices - 1, 0.0, face)
        tail_kappa = jnp.where(device == devices - 1, 0.0, tail_kappa)
    lower = -face * tail_u
    upper = -tail_kappa * next_of(head_w)
    diagonal = 1.0 + tail_kappa * next_of(head_u) + face * tail_w
    return circular_solve(
        lower, upper, diagonal + lower + upper, tail_kappa * next_of(head_p) - face * tail_p
    )


def interface_flux(edge, axis, mesh_axis, periodic, exchange):
    terms = lax.slice_in_dim(edge, 0, TERMS, axis=axis) if edge.shape[axis] > TERMS else edge
    devices = lax.axis_size(mesh_axis)
    if exchange == "all_to_all":
        copies = jnp.broadcast_to(terms[None], (devices,) + terms.shape)
        gathered = lax.all_to_all(copies, mesh_axis, 0, 0, tiled=True)
    else:
        gathered = lax.all_gather(terms[None], mesh_axis, axis=0, tiled=True)
    terms = [lax.index_in_dim(gathered, k, axis + 1, keepdims=False) for k in range(TERMS)]
    flux = flux_system(terms, periodic)
    index = lax.axis_index(mesh_axis)
    here = lax.dynamic_index_in_dim(flux, index, 0, keepdims=True)
    before = lax.dynamic_index_in_dim(flux, (index + devices - 1) % devices, 0, keepdims=True)
    return before[0], here[0]


def lon_flux(edge):
    devices = lax.axis_size("lon")
    copies = jnp.broadcast_to(edge[None], (devices,) + edge.shape)
    gathered = lax.all_to_all(copies, "lon", 0, 0, tiled=True)
    terms = [gathered[:, k] for k in range(TERMS)]
    flux = flux_system(terms, True)
    index = lax.axis_index("lon")
    here = lax.dynamic_index_in_dim(flux, index, 0, keepdims=False)
    before = lax.dynamic_index_in_dim(flux, (index + devices - 1) % devices, 0, keepdims=False)
    return before, here


def shards(source, kappa_lon, kappa_lat, sea_mask):
    p_lon, u_lon, w_lon, edge_lon = lon_pass(source, kappa_lon, sea_mask)
    u_lat, w_lat, left, right, diagonal, matrix_edge, scale = lat_matrix(kappa_lat, sea_mask, kappa_lon)
    before, here = lon_flux(edge_lon)
    lines = source.shape[:2] + (1,)
    flux = jnp.stack([before.reshape(lines), here.reshape(lines)], 0)
    p_lat, edge_lat = lat_rhs(
        p_lon, u_lon, w_lon, flux, sea_mask, left, right, diagonal, matrix_edge,
    )
    before, here = interface_flux(edge_lat, 0, "lat", False, "all_gather")
    return scale * (p_lat - u_lat * before[:, None, :] + w_lat * here[:, None, :])


def solution(mesh):
    return jax.shard_map(
        shards,
        mesh=mesh,
        in_specs=(
            P(None, "lat", "lon"),
            P(None, "lat", "lon"),
            P(None, "lat", "lon"),
            P(None, "lat", "lon"),
        ),
        out_specs=P(None, "lat", "lon"),
        check_vma=False,
    )
```

```python
import functools

import jax
import jax.numpy as jnp
from jax import lax
from jax.experimental import pallas as pl
from jax.experimental.pallas import tpu as pltpu
from jax.sharding import PartitionSpec as P

TERMS = 7


def shifted(values, shift, axis):
    length = values.shape[axis]
    return pltpu.roll(values, shift % length, axis)


def block_solve(lower_band, upper_band, excess, sources, axis, weights=None):
    length = lower_band.shape[axis]
    stride = 1
    while stride < length:
        inverse = 1.0 / (excess - lower_band - upper_band)
        left_weight = -lower_band * shifted(inverse, stride, axis)
        right_coefficient = -upper_band * shifted(inverse, -stride, axis)
        if weights is not None:
            weights.append((left_weight, right_coefficient))
        new_lower = left_weight * shifted(lower_band, stride, axis)
        new_upper = right_coefficient * shifted(upper_band, -stride, axis)
        excess = (
            excess
            + left_weight * shifted(excess, stride, axis)
            + right_coefficient * shifted(excess, -stride, axis)
        )
        sources = [
            member
            + left_weight * shifted(member, stride, axis)
            + right_coefficient * shifted(member, -stride, axis)
            for member in sources
        ]
        lower_band, upper_band = (new_lower, new_upper)
        stride = stride * 2
    diagonal = excess - lower_band - upper_band
    if weights is not None:
        weights.append(diagonal)
    return [member / diagonal for member in sources]


def pass_kernel(axis, corrected, *refs):
    if corrected:
        (p_ref, u_ref, w_ref, before_ref, here_ref, kappa_ref, mask_ref,
         p_out, u_out, w_out, edge_out) = refs
        values = (
            p_ref[...]
            - u_ref[...] * before_ref[...]
            + w_ref[...] * here_ref[...]
        )
    else:
        (source_ref, kappa_ref, mask_ref, p_out, u_out, w_out, edge_out) = refs
        values = source_ref[...]
    shape = values.shape
    length = shape[axis]
    wet = mask_ref[...].astype(jnp.float32)
    weight = kappa_ref[...].astype(jnp.float32) * wet
    position = lax.broadcasted_iota(jnp.int32, shape, axis)
    last = position == length - 1
    right_face = jnp.where(last, 0.0, weight * shifted(wet, -1, axis))
    left_face = shifted(right_face, 1, axis)
    first = position == 0
    particular, from_left, from_right = block_solve(
        -left_face,
        -right_face,
        jnp.ones(shape, jnp.float32),
        [values, jnp.where(first, 1.0, 0.0), jnp.where(last, 1.0, 0.0)],
        axis,
    )
    p_out[...] = particular
    u_out[...] = from_left
    w_out[...] = from_right
    tail_weight = shifted(weight, 4, axis)
    entries = [
        wet * particular,
        shifted(wet * from_left, 1, axis),
        shifted(wet * from_right, 2, axis),
        tail_weight,
        shifted(from_left, 4 + 1, axis),
        shifted(from_right, 4 + 2, axis),
        shifted(particular, 4 + 3, axis),
    ]
    edge = entries[0]
    for k in range(1, TERMS):
        edge = jnp.where(position == k, entries[k], edge)
    if axis == 2:
        edge_out[...] = edge
    else:
        edge_out[...] = lax.slice_in_dim(edge, 0, 8, axis=axis)


def local_pass(axis, inputs):
    shape = inputs[0].shape
    corrected = len(inputs) > 3
    edge_shape = shape if axis == 2 else shape[:axis] + (8,) + shape[axis + 1:]
    return pl.pallas_call(
        functools.partial(pass_kernel, axis, corrected),
        out_shape=(
            jax.ShapeDtypeStruct(shape, jnp.float32),
            jax.ShapeDtypeStruct(shape, jnp.float32),
            jax.ShapeDtypeStruct(shape, jnp.float32),
            jax.ShapeDtypeStruct(edge_shape, jnp.float32),
        ),
    )(*inputs)


def lon_kernel(source_ref, kappa_ref, mask_ref, p_out, u_out, w_out, edge_out):
    levels, rows, length = source_ref.shape
    lines = levels * rows

    def across(values):
        return jnp.transpose(values.astype(jnp.float32).reshape(lines, length))

    def back(values):
        return jnp.transpose(values).reshape(levels, rows, length)

    wet = across(mask_ref[...])
    weight = across(kappa_ref[...]) * wet
    values = across(source_ref[...])
    axis = 0
    shape = values.shape
    position = lax.broadcasted_iota(jnp.int32, shape, axis)
    last = position == length - 1
    right_face = jnp.where(last, 0.0, weight * shifted(wet, -1, axis))
    left_face = shifted(right_face, 1, axis)
    particular, from_left, from_right = block_solve(
        -left_face,
        -right_face,
        jnp.ones(shape, jnp.float32),
        [values, jnp.where(position == 0, 1.0, 0.0), jnp.where(last, 1.0, 0.0)],
        axis,
    )
    p_out[...] = back(particular)
    u_out[...] = back(from_left)
    w_out[...] = back(from_right)
    head_wet = wet[0:1, :]
    rows = [
        head_wet * particular[0:1, :],
        head_wet * from_left[0:1, :],
        head_wet * from_right[0:1, :],
        weight[length - 1:length, :],
        from_left[length - 1:length, :],
        from_right[length - 1:length, :],
        particular[length - 1:length, :],
    ]
    for copy in range(edge_out.shape[0]):
        for k, row in enumerate(rows):
            edge_out[copy, k:k + 1, :] = row


def lon_pass(source, kappa_lon, sea_mask, devices):
    shape = source.shape
    full = jax.ShapeDtypeStruct(shape, jnp.float32)
    edge = jax.ShapeDtypeStruct((devices, TERMS, shape[0] * shape[1]), jnp.float32)
    return pl.pallas_call(lon_kernel, out_shape=(full, full, full, edge))(source, kappa_lon, sea_mask)


def lat_matrix_kernel(kappa_ref, mask_ref, lon_kappa_ref, u_out, w_out, left_out, right_out,
                      diagonal_out, edge_out, scale_out, weight_scratch):
    axis = 1
    wet = mask_ref[...].astype(jnp.float32)
    lat_kappa = kappa_ref[...].astype(jnp.float32)
    scale_out[...] = wet * 4.0 * jnp.sqrt(jnp.sqrt(lon_kappa_ref[...].astype(jnp.float32) * lat_kappa))
    weight = lat_kappa * wet
    shape = wet.shape
    length = shape[axis]
    position = lax.broadcasted_iota(jnp.int32, shape, axis)
    last = position == length - 1
    right_face = jnp.where(last, 0.0, weight * shifted(wet, -1, axis))
    left_face = shifted(right_face, 1, axis)
    weights = []
    from_left, from_right = block_solve(
        -left_face,
        -right_face,
        jnp.ones(shape, jnp.float32),
        [jnp.where(position == 0, 1.0, 0.0), jnp.where(last, 1.0, 0.0)],
        axis,
        weights,
    )
    u_out[...] = from_left
    w_out[...] = from_right
    for step, (left_weight, right_coefficient) in enumerate(weights[:-1]):
        left_out[step] = left_weight
        right_out[step] = right_coefficient
    diagonal_out[...] = weights[-1]
    weight_scratch[...] = weight
    head_wet = mask_ref[:, 0, :].astype(jnp.float32)
    edge_out[0] = head_wet * u_out[:, 0, :]
    edge_out[1] = head_wet * w_out[:, 0, :]
    edge_out[2] = weight_scratch[:, length - 1, :]
    edge_out[3] = u_out[:, length - 1, :]
    edge_out[4] = w_out[:, length - 1, :]


def lat_rhs_kernel(p_ref, u_ref, w_ref, flux_ref, mask_ref, left_ref, right_ref,
                   diagonal_ref, matrix_edge_ref, p_out, edge_out):
    axis = 1
    values = p_ref[...] - u_ref[...] * flux_ref[0] + w_ref[...] * flux_ref[1]
    length = values.shape[axis]
    stride = 1
    step = 0
    while stride < length:
        values = (
            values
            + left_ref[step] * shifted(values, stride, axis)
            + right_ref[step] * shifted(values, -stride, axis)
        )
        stride = stride * 2
        step = step + 1
    p_out[...] = values / diagonal_ref[...]
    edge_out[0] = mask_ref[:, 0, :].astype(jnp.float32) * p_out[:, 0, :]
    edge_out[1:TERMS - 1] = matrix_edge_ref[...]
    edge_out[TERMS - 1] = p_out[:, length - 1, :]


def lat_matrix(kappa_lat, sea_mask, kappa_lon):
    shape = kappa_lat.shape
    steps = (shape[1] - 1).bit_length()
    full = jax.ShapeDtypeStruct(shape, jnp.float32)
    stacked = jax.ShapeDtypeStruct((steps,) + shape, jnp.float32)
    edge = jax.ShapeDtypeStruct((TERMS - 2, shape[0], shape[2]), jnp.float32)
    return pl.pallas_call(
        lat_matrix_kernel,
        out_shape=(full, full, stacked, stacked, full, edge, full),
        scratch_shapes=[pltpu.VMEM(shape, jnp.float32)],
    )(kappa_lat, sea_mask, kappa_lon)


def lat_rhs(*inputs):
    shape = inputs[0].shape
    return pl.pallas_call(
        lat_rhs_kernel,
        out_shape=(
            jax.ShapeDtypeStruct(shape, jnp.float32),
            jax.ShapeDtypeStruct((TERMS, shape[0], shape[2]), jnp.float32),
        ),
    )(*inputs)


def circular_solve(lower_band, upper_band, excess, sources):
    devices = lower_band.shape[0]
    stride = 1
    while stride < devices:
        inverse = 1.0 / (excess - lower_band - upper_band)
        left_weight = -lower_band * jnp.roll(inverse, stride, 0)
        right_coefficient = -upper_band * jnp.roll(inverse, -stride, 0)
        new_lower = left_weight * jnp.roll(lower_band, stride, 0)
        new_upper = right_coefficient * jnp.roll(upper_band, -stride, 0)
        excess = (
            excess
            + left_weight * jnp.roll(excess, stride, 0)
            + right_coefficient * jnp.roll(excess, -stride, 0)
        )
        sources = (
            sources
            + left_weight * jnp.roll(sources, stride, 0)
            + right_coefficient * jnp.roll(sources, -stride, 0)
        )
        lower_band, upper_band = (new_lower, new_upper)
        stride = stride * 2
    return sources / excess


def flux_system(terms, periodic):
    head_p, head_u, head_w, tail_kappa, tail_u, tail_w, tail_p = terms
    devices = head_p.shape[0]

    def next_of(member):
        return jnp.roll(member, -1, 0)

    next_wet = jnp.where(next_of(head_u) > 0.0, 1.0, 0.0)
    face = tail_kappa * next_wet
    if not periodic:
        device = lax.broadcasted_iota(jnp.int32, face.shape, 0)
        face = jnp.where(device == devices - 1, 0.0, face)
        tail_kappa = jnp.where(device == devices - 1, 0.0, tail_kappa)
    lower = -face * tail_u
    upper = -tail_kappa * next_of(head_w)
    diagonal = 1.0 + tail_kappa * next_of(head_u) + face * tail_w
    return circular_solve(
        lower, upper, diagonal + lower + upper, tail_kappa * next_of(head_p) - face * tail_p
    )


def interface_flux(edge, axis, mesh_axis, periodic, exchange):
    terms = lax.slice_in_dim(edge, 0, TERMS, axis=axis) if edge.shape[axis] > TERMS else edge
    devices = lax.axis_size(mesh_axis)
    if exchange == "all_to_all":
        copies = jnp.broadcast_to(terms[None], (devices,) + terms.shape)
        gathered = lax.all_to_all(copies, mesh_axis, 0, 0, tiled=True)
    else:
        gathered = lax.all_gather(terms[None], mesh_axis, axis=0, tiled=True)
    terms = [lax.index_in_dim(gathered, k, axis + 1, keepdims=False) for k in range(TERMS)]
    flux = flux_system(terms, periodic)
    index = lax.axis_index(mesh_axis)
    here = lax.dynamic_index_in_dim(flux, index, 0, keepdims=True)
    before = lax.dynamic_index_in_dim(flux, (index + devices - 1) % devices, 0, keepdims=True)
    return before[0], here[0]


def lon_flux(copies):
    devices = copies.shape[0]
    gathered = lax.all_to_all(copies, "lon", 0, 0, tiled=True)
    terms = [gathered[:, k] for k in range(TERMS)]
    flux = flux_system(terms, True)
    index = lax.axis_index("lon")
    here = lax.dynamic_index_in_dim(flux, index, 0, keepdims=False)
    before = lax.dynamic_index_in_dim(flux, (index + devices - 1) % devices, 0, keepdims=False)
    return before, here


def shards(source, kappa_lon, kappa_lat, sea_mask):
    p_lon, u_lon, w_lon, edge_lon = lon_pass(source, kappa_lon, sea_mask, lax.axis_size("lon"))
    u_lat, w_lat, left, right, diagonal, matrix_edge, scale = lat_matrix(kappa_lat, sea_mask, kappa_lon)
    before, here = lon_flux(edge_lon)
    lines = source.shape[:2] + (1,)
    flux = jnp.stack([before.reshape(lines), here.reshape(lines)], 0)
    p_lat, edge_lat = lat_rhs(
        p_lon, u_lon, w_lon, flux, sea_mask, left, right, diagonal, matrix_edge,
    )
    before, here = interface_flux(edge_lat, 0, "lat", False, "all_gather")
    return scale * (p_lat - u_lat * before[:, None, :] + w_lat * here[:, None, :])


def solution(mesh):
    return jax.shard_map(
        shards,
        mesh=mesh,
        in_specs=(
            P(None, "lat", "lon"),
            P(None, "lat", "lon"),
            P(None, "lat", "lon"),
            P(None, "lat", "lon"),
        ),
        out_specs=P(None, "lat", "lon"),
        check_vma=False,
    )
```

```python
import functools

import jax
import jax.numpy as jnp
from jax import lax
from jax.experimental import pallas as pl
from jax.experimental.pallas import tpu as pltpu
from jax.sharding import PartitionSpec as P

TERMS = 7


def shifted(values, shift, axis):
    length = values.shape[axis]
    return pltpu.roll(values, shift % length, axis)


def block_solve(lower_band, upper_band, excess, sources, axis, weights=None):
    length = lower_band.shape[axis]
    stride = 1
    while stride < length:
        inverse = 1.0 / (excess - lower_band - upper_band)
        left_weight = -lower_band * shifted(inverse, stride, axis)
        right_coefficient = -upper_band * shifted(inverse, -stride, axis)
        if weights is not None:
            weights.append((left_weight, right_coefficient))
        new_lower = left_weight * shifted(lower_band, stride, axis)
        new_upper = right_coefficient * shifted(upper_band, -stride, axis)
        excess = (
            excess
            + left_weight * shifted(excess, stride, axis)
            + right_coefficient * shifted(excess, -stride, axis)
        )
        sources = [
            member
            + left_weight * shifted(member, stride, axis)
            + right_coefficient * shifted(member, -stride, axis)
            for member in sources
        ]
        lower_band, upper_band = (new_lower, new_upper)
        stride = stride * 2
    diagonal = excess - lower_band - upper_band
    if weights is not None:
        weights.append(diagonal)
    return [member / diagonal for member in sources]


def pass_kernel(axis, corrected, *refs):
    if corrected:
        (p_ref, u_ref, w_ref, before_ref, here_ref, kappa_ref, mask_ref,
         p_out, u_out, w_out, edge_out) = refs
        values = (
            p_ref[...]
            - u_ref[...] * before_ref[...]
            + w_ref[...] * here_ref[...]
        )
    else:
        (source_ref, kappa_ref, mask_ref, p_out, u_out, w_out, edge_out) = refs
        values = source_ref[...]
    shape = values.shape
    length = shape[axis]
    wet = mask_ref[...].astype(jnp.float32)
    weight = kappa_ref[...].astype(jnp.float32) * wet
    position = lax.broadcasted_iota(jnp.int32, shape, axis)
    last = position == length - 1
    right_face = jnp.where(last, 0.0, weight * shifted(wet, -1, axis))
    left_face = shifted(right_face, 1, axis)
    first = position == 0
    particular, from_left, from_right = block_solve(
        -left_face,
        -right_face,
        jnp.ones(shape, jnp.float32),
        [values, jnp.where(first, 1.0, 0.0), jnp.where(last, 1.0, 0.0)],
        axis,
    )
    p_out[...] = particular
    u_out[...] = from_left
    w_out[...] = from_right
    tail_weight = shifted(weight, 4, axis)
    entries = [
        wet * particular,
        shifted(wet * from_left, 1, axis),
        shifted(wet * from_right, 2, axis),
        tail_weight,
        shifted(from_left, 4 + 1, axis),
        shifted(from_right, 4 + 2, axis),
        shifted(particular, 4 + 3, axis),
    ]
    edge = entries[0]
    for k in range(1, TERMS):
        edge = jnp.where(position == k, entries[k], edge)
    if axis == 2:
        edge_out[...] = edge
    else:
        edge_out[...] = lax.slice_in_dim(edge, 0, 8, axis=axis)


def local_pass(axis, inputs):
    shape = inputs[0].shape
    corrected = len(inputs) > 3
    edge_shape = shape if axis == 2 else shape[:axis] + (8,) + shape[axis + 1:]
    return pl.pallas_call(
        functools.partial(pass_kernel, axis, corrected),
        out_shape=(
            jax.ShapeDtypeStruct(shape, jnp.float32),
            jax.ShapeDtypeStruct(shape, jnp.float32),
            jax.ShapeDtypeStruct(shape, jnp.float32),
            jax.ShapeDtypeStruct(edge_shape, jnp.float32),
        ),
    )(*inputs)


def lon_kernel(source_ref, kappa_ref, mask_ref, p_out, u_out, w_out, edge_out):
    levels, rows, length = source_ref.shape
    lines = levels * rows

    def across(values):
        return jnp.transpose(values.astype(jnp.float32).reshape(lines, length))

    def back(values):
        return jnp.transpose(values).reshape(levels, rows, length)

    wet = across(mask_ref[...])
    weight = across(kappa_ref[...]) * wet
    values = across(source_ref[...])
    axis = 0
    shape = values.shape
    position = lax.broadcasted_iota(jnp.int32, shape, axis)
    last = position == length - 1
    right_face = jnp.where(last, 0.0, weight * shifted(wet, -1, axis))
    left_face = shifted(right_face, 1, axis)
    particular, from_left, from_right = block_solve(
        -left_face,
        -right_face,
        jnp.ones(shape, jnp.float32),
        [values, jnp.where(position == 0, 1.0, 0.0), jnp.where(last, 1.0, 0.0)],
        axis,
    )
    p_out[...] = back(particular)
    u_out[...] = back(from_left)
    w_out[...] = back(from_right)
    head_wet = wet[0:1, :]
    rows = [
        head_wet * particular[0:1, :],
        head_wet * from_left[0:1, :],
        head_wet * from_right[0:1, :],
        weight[length - 1:length, :],
        from_left[length - 1:length, :],
        from_right[length - 1:length, :],
        particular[length - 1:length, :],
    ]
    for copy in range(edge_out.shape[0]):
        for k, row in enumerate(rows):
            edge_out[copy, k:k + 1, :] = row


def lon_pass(source, kappa_lon, sea_mask, devices):
    shape = source.shape
    full = jax.ShapeDtypeStruct(shape, jnp.float32)
    edge = jax.ShapeDtypeStruct((devices, TERMS, shape[0] * shape[1]), jnp.float32)
    return pl.pallas_call(lon_kernel, out_shape=(full, full, full, edge))(source, kappa_lon, sea_mask)


def lat_matrix_kernel(kappa_ref, mask_ref, lon_kappa_ref, u_out, w_out, left_out, right_out,
                      diagonal_out, edge_out, scale_out, weight_scratch):
    axis = 1
    wet = mask_ref[...].astype(jnp.float32)
    lat_kappa = kappa_ref[...].astype(jnp.float32)
    scale_out[...] = wet * 4.0 * jnp.sqrt(jnp.sqrt(lon_kappa_ref[...].astype(jnp.float32) * lat_kappa))
    weight = lat_kappa * wet
    shape = wet.shape
    length = shape[axis]
    position = lax.broadcasted_iota(jnp.int32, shape, axis)
    last = position == length - 1
    right_face = jnp.where(last, 0.0, weight * shifted(wet, -1, axis))
    left_face = shifted(right_face, 1, axis)
    weights = []
    from_left, from_right = block_solve(
        -left_face,
        -right_face,
        jnp.ones(shape, jnp.float32),
        [jnp.where(position == 0, 1.0, 0.0), jnp.where(last, 1.0, 0.0)],
        axis,
        weights,
    )
    u_out[...] = from_left
    w_out[...] = from_right
    for step, (left_weight, right_coefficient) in enumerate(weights[:-1]):
        left_out[step] = left_weight
        right_out[step] = right_coefficient
    diagonal_out[...] = weights[-1]
    weight_scratch[...] = weight
    head_wet = mask_ref[:, 0, :].astype(jnp.float32)
    edge_out[0] = head_wet * u_out[:, 0, :]
    edge_out[1] = head_wet * w_out[:, 0, :]
    edge_out[2] = weight_scratch[:, length - 1, :]
    edge_out[3] = u_out[:, length - 1, :]
    edge_out[4] = w_out[:, length - 1, :]


def lat_rhs_kernel(p_ref, u_ref, w_ref, flux_ref, mask_ref, left_ref, right_ref,
                   diagonal_ref, matrix_edge_ref, p_out, edge_out):
    axis = 1
    levels, rows, width = p_ref.shape
    lines = flux_ref.shape[1]
    padded = jnp.concatenate(
        [flux_ref[...], jnp.zeros((width - flux_ref.shape[0], lines), jnp.float32)], 0
    )
    columns = jnp.transpose(padded)
    before = columns[:, 0:1].reshape(levels, rows, 1)
    here = columns[:, 1:2].reshape(levels, rows, 1)
    values = p_ref[...] - u_ref[...] * before + w_ref[...] * here
    length = values.shape[axis]
    stride = 1
    step = 0
    while stride < length:
        values = (
            values
            + left_ref[step] * shifted(values, stride, axis)
            + right_ref[step] * shifted(values, -stride, axis)
        )
        stride = stride * 2
        step = step + 1
    p_out[...] = values / diagonal_ref[...]
    edge_out[0] = mask_ref[:, 0, :].astype(jnp.float32) * p_out[:, 0, :]
    edge_out[1:TERMS - 1] = matrix_edge_ref[...]
    edge_out[TERMS - 1] = p_out[:, length - 1, :]


def lat_matrix(kappa_lat, sea_mask, kappa_lon):
    shape = kappa_lat.shape
    steps = (shape[1] - 1).bit_length()
    full = jax.ShapeDtypeStruct(shape, jnp.float32)
    stacked = jax.ShapeDtypeStruct((steps,) + shape, jnp.float32)
    edge = jax.ShapeDtypeStruct((TERMS - 2, shape[0], shape[2]), jnp.float32)
    return pl.pallas_call(
        lat_matrix_kernel,
        out_shape=(full, full, stacked, stacked, full, edge, full),
        scratch_shapes=[pltpu.VMEM(shape, jnp.float32)],
    )(kappa_lat, sea_mask, kappa_lon)


def lat_rhs(*inputs):
    shape = inputs[0].shape
    return pl.pallas_call(
        lat_rhs_kernel,
        out_shape=(
            jax.ShapeDtypeStruct(shape, jnp.float32),
            jax.ShapeDtypeStruct((TERMS, shape[0], shape[2]), jnp.float32),
        ),
    )(*inputs)


def circular_solve(lower_band, upper_band, excess, sources):
    devices = lower_band.shape[0]
    stride = 1
    while stride < devices:
        inverse = 1.0 / (excess - lower_band - upper_band)
        left_weight = -lower_band * jnp.roll(inverse, stride, 0)
        right_coefficient = -upper_band * jnp.roll(inverse, -stride, 0)
        new_lower = left_weight * jnp.roll(lower_band, stride, 0)
        new_upper = right_coefficient * jnp.roll(upper_band, -stride, 0)
        excess = (
            excess
            + left_weight * jnp.roll(excess, stride, 0)
            + right_coefficient * jnp.roll(excess, -stride, 0)
        )
        sources = (
            sources
            + left_weight * jnp.roll(sources, stride, 0)
            + right_coefficient * jnp.roll(sources, -stride, 0)
        )
        lower_band, upper_band = (new_lower, new_upper)
        stride = stride * 2
    return sources / excess


def flux_system(terms, periodic):
    head_p, head_u, head_w, tail_kappa, tail_u, tail_w, tail_p = terms
    devices = head_p.shape[0]

    def next_of(member):
        return jnp.roll(member, -1, 0)

    next_wet = jnp.where(next_of(head_u) > 0.0, 1.0, 0.0)
    face = tail_kappa * next_wet
    if not periodic:
        device = lax.broadcasted_iota(jnp.int32, face.shape, 0)
        face = jnp.where(device == devices - 1, 0.0, face)
        tail_kappa = jnp.where(device == devices - 1, 0.0, tail_kappa)
    lower = -face * tail_u
    upper = -tail_kappa * next_of(head_w)
    diagonal = 1.0 + tail_kappa * next_of(head_u) + face * tail_w
    return circular_solve(
        lower, upper, diagonal + lower + upper, tail_kappa * next_of(head_p) - face * tail_p
    )


def interface_flux(edge, axis, mesh_axis, periodic, exchange):
    terms = lax.slice_in_dim(edge, 0, TERMS, axis=axis) if edge.shape[axis] > TERMS else edge
    devices = lax.axis_size(mesh_axis)
    if exchange == "all_to_all":
        copies = jnp.broadcast_to(terms[None], (devices,) + terms.shape)
        gathered = lax.all_to_all(copies, mesh_axis, 0, 0, tiled=True)
    else:
        gathered = lax.all_gather(terms[None], mesh_axis, axis=0, tiled=True)
    terms = [lax.index_in_dim(gathered, k, axis + 1, keepdims=False) for k in range(TERMS)]
    flux = flux_system(terms, periodic)
    index = lax.axis_index(mesh_axis)
    here = lax.dynamic_index_in_dim(flux, index, 0, keepdims=True)
    before = lax.dynamic_index_in_dim(flux, (index + devices - 1) % devices, 0, keepdims=True)
    return before[0], here[0]


def lon_flux(copies):
    devices = copies.shape[0]
    gathered = lax.all_to_all(copies, "lon", 0, 0, tiled=True)
    terms = [gathered[:, k] for k in range(TERMS)]
    flux = flux_system(terms, True)
    index = lax.axis_index("lon")
    here = lax.dynamic_index_in_dim(flux, index, 0, keepdims=False)
    before = lax.dynamic_index_in_dim(flux, (index + devices - 1) % devices, 0, keepdims=False)
    return before, here


def shards(source, kappa_lon, kappa_lat, sea_mask):
    p_lon, u_lon, w_lon, edge_lon = lon_pass(source, kappa_lon, sea_mask, lax.axis_size("lon"))
    u_lat, w_lat, left, right, diagonal, matrix_edge, scale = lat_matrix(kappa_lat, sea_mask, kappa_lon)
    before, here = lon_flux(edge_lon)
    flux = jnp.concatenate([before[None], here[None], jnp.zeros((6,) + before.shape, jnp.float32)], 0)
    p_lat, edge_lat = lat_rhs(
        p_lon, u_lon, w_lon, flux, sea_mask, left, right, diagonal, matrix_edge,
    )
    before, here = interface_flux(edge_lat, 0, "lat", False, "all_gather")
    return scale * (p_lat - u_lat * before[:, None, :] + w_lat * here[:, None, :])


def solution(mesh):
    return jax.shard_map(
        shards,
        mesh=mesh,
        in_specs=(
            P(None, "lat", "lon"),
            P(None, "lat", "lon"),
            P(None, "lat", "lon"),
            P(None, "lat", "lon"),
        ),
        out_specs=P(None, "lat", "lon"),
        check_vma=False,
    )
```

```python
import functools

import jax
import jax.numpy as jnp
from jax import lax
from jax.experimental import pallas as pl
from jax.experimental.pallas import tpu as pltpu
from jax.sharding import PartitionSpec as P

TERMS = 7


def shifted(values, shift, axis):
    length = values.shape[axis]
    return pltpu.roll(values, shift % length, axis)


def block_solve(lower_band, upper_band, excess, sources, axis, weights=None):
    length = lower_band.shape[axis]
    stride = 1
    while stride < length:
        inverse = 1.0 / (excess - lower_band - upper_band)
        left_weight = -lower_band * shifted(inverse, stride, axis)
        right_coefficient = -upper_band * shifted(inverse, -stride, axis)
        if weights is not None:
            weights.append((left_weight, right_coefficient))
        new_lower = left_weight * shifted(lower_band, stride, axis)
        new_upper = right_coefficient * shifted(upper_band, -stride, axis)
        excess = (
            excess
            + left_weight * shifted(excess, stride, axis)
            + right_coefficient * shifted(excess, -stride, axis)
        )
        sources = [
            member
            + left_weight * shifted(member, stride, axis)
            + right_coefficient * shifted(member, -stride, axis)
            for member in sources
        ]
        lower_band, upper_band = (new_lower, new_upper)
        stride = stride * 2
    diagonal = excess - lower_band - upper_band
    if weights is not None:
        weights.append(diagonal)
    return [member / diagonal for member in sources]


def pass_kernel(axis, corrected, *refs):
    if corrected:
        (p_ref, u_ref, w_ref, before_ref, here_ref, kappa_ref, mask_ref,
         p_out, u_out, w_out, edge_out) = refs
        values = (
            p_ref[...]
            - u_ref[...] * before_ref[...]
            + w_ref[...] * here_ref[...]
        )
    else:
        (source_ref, kappa_ref, mask_ref, p_out, u_out, w_out, edge_out) = refs
        values = source_ref[...]
    shape = values.shape
    length = shape[axis]
    wet = mask_ref[...].astype(jnp.float32)
    weight = kappa_ref[...].astype(jnp.float32) * wet
    position = lax.broadcasted_iota(jnp.int32, shape, axis)
    last = position == length - 1
    right_face = jnp.where(last, 0.0, weight * shifted(wet, -1, axis))
    left_face = shifted(right_face, 1, axis)
    first = position == 0
    particular, from_left, from_right = block_solve(
        -left_face,
        -right_face,
        jnp.ones(shape, jnp.float32),
        [values, jnp.where(first, 1.0, 0.0), jnp.where(last, 1.0, 0.0)],
        axis,
    )
    p_out[...] = particular
    u_out[...] = from_left
    w_out[...] = from_right
    tail_weight = shifted(weight, 4, axis)
    entries = [
        wet * particular,
        shifted(wet * from_left, 1, axis),
        shifted(wet * from_right, 2, axis),
        tail_weight,
        shifted(from_left, 4 + 1, axis),
        shifted(from_right, 4 + 2, axis),
        shifted(particular, 4 + 3, axis),
    ]
    edge = entries[0]
    for k in range(1, TERMS):
        edge = jnp.where(position == k, entries[k], edge)
    if axis == 2:
        edge_out[...] = edge
    else:
        edge_out[...] = lax.slice_in_dim(edge, 0, 8, axis=axis)


def local_pass(axis, inputs):
    shape = inputs[0].shape
    corrected = len(inputs) > 3
    edge_shape = shape if axis == 2 else shape[:axis] + (8,) + shape[axis + 1:]
    return pl.pallas_call(
        functools.partial(pass_kernel, axis, corrected),
        out_shape=(
            jax.ShapeDtypeStruct(shape, jnp.float32),
            jax.ShapeDtypeStruct(shape, jnp.float32),
            jax.ShapeDtypeStruct(shape, jnp.float32),
            jax.ShapeDtypeStruct(edge_shape, jnp.float32),
        ),
    )(*inputs)


def lon_kernel(source_ref, kappa_ref, mask_ref, p_out, u_out, w_out, edge_out):
    levels, rows, length = source_ref.shape
    lines = levels * rows

    def across(values):
        return jnp.transpose(values.astype(jnp.float32).reshape(lines, length))

    def back(values):
        return jnp.transpose(values).reshape(levels, rows, length)

    wet = across(mask_ref[...])
    weight = across(kappa_ref[...]) * wet
    values = across(source_ref[...])
    axis = 0
    shape = values.shape
    position = lax.broadcasted_iota(jnp.int32, shape, axis)
    last = position == length - 1
    right_face = jnp.where(last, 0.0, weight * shifted(wet, -1, axis))
    left_face = shifted(right_face, 1, axis)
    particular, from_left, from_right = block_solve(
        -left_face,
        -right_face,
        jnp.ones(shape, jnp.float32),
        [values, jnp.where(position == 0, 1.0, 0.0), jnp.where(last, 1.0, 0.0)],
        axis,
    )
    p_out[...] = back(particular)
    u_out[...] = back(from_left)
    w_out[...] = back(from_right)
    head_wet = wet[0:1, :]
    rows = [
        head_wet * particular[0:1, :],
        head_wet * from_left[0:1, :],
        head_wet * from_right[0:1, :],
        weight[length - 1:length, :],
        from_left[length - 1:length, :],
        from_right[length - 1:length, :],
        particular[length - 1:length, :],
    ]
    for copy in range(edge_out.shape[0]):
        for k, row in enumerate(rows):
            edge_out[copy, k:k + 1, :] = row


def lon_pass(source, kappa_lon, sea_mask, devices):
    shape = source.shape
    full = jax.ShapeDtypeStruct(shape, jnp.float32)
    edge = jax.ShapeDtypeStruct((devices, TERMS, shape[0] * shape[1]), jnp.float32)
    return pl.pallas_call(lon_kernel, out_shape=(full, full, full, edge))(source, kappa_lon, sea_mask)


def lat_matrix_kernel(kappa_ref, mask_ref, lon_kappa_ref, u_out, w_out, edge_out, scale_out,
                      weight_scratch):
    axis = 1
    wet, weight, position, left_face, right_face = lat_faces(kappa_ref, mask_ref, axis)
    lat_kappa = kappa_ref[...].astype(jnp.float32)
    scale_out[...] = wet * 4.0 * jnp.sqrt(jnp.sqrt(lon_kappa_ref[...].astype(jnp.float32) * lat_kappa))
    shape = wet.shape
    length = shape[axis]
    from_left, from_right = block_solve(
        -left_face,
        -right_face,
        jnp.ones(shape, jnp.float32),
        [jnp.where(position == 0, 1.0, 0.0), jnp.where(position == length - 1, 1.0, 0.0)],
        axis,
    )
    u_out[...] = from_left
    w_out[...] = from_right
    weight_scratch[...] = weight
    head_wet = mask_ref[:, 0, :].astype(jnp.float32)
    edge_out[0] = head_wet * u_out[:, 0, :]
    edge_out[1] = head_wet * w_out[:, 0, :]
    edge_out[2] = weight_scratch[:, length - 1, :]
    edge_out[3] = u_out[:, length - 1, :]
    edge_out[4] = w_out[:, length - 1, :]


def lat_faces(kappa_ref, mask_ref, axis):
    wet = mask_ref[...].astype(jnp.float32)
    weight = kappa_ref[...].astype(jnp.float32) * wet
    position = lax.broadcasted_iota(jnp.int32, wet.shape, axis)
    last = position == wet.shape[axis] - 1
    right_face = jnp.where(last, 0.0, weight * shifted(wet, -1, axis))
    left_face = shifted(right_face, 1, axis)
    return wet, weight, position, left_face, right_face


def lat_rhs_kernel(p_ref, u_ref, w_ref, flux_ref, kappa_ref, mask_ref, matrix_edge_ref,
                   p_out, edge_out):
    axis = 1
    levels, rows, width = p_ref.shape
    lines = flux_ref.shape[1]
    padded = jnp.concatenate(
        [flux_ref[...], jnp.zeros((width - flux_ref.shape[0], lines), jnp.float32)], 0
    )
    columns = jnp.transpose(padded)
    before = columns[:, 0:1].reshape(levels, rows, 1)
    here = columns[:, 1:2].reshape(levels, rows, 1)
    values = p_ref[...] - u_ref[...] * before + w_ref[...] * here
    wet, weight, position, left_face, right_face = lat_faces(kappa_ref, mask_ref, axis)
    (particular,) = block_solve(
        -left_face, -right_face, jnp.ones(values.shape, jnp.float32), [values], axis
    )
    p_out[...] = particular
    length = values.shape[axis]
    edge_out[0] = mask_ref[:, 0, :].astype(jnp.float32) * p_out[:, 0, :]
    edge_out[1:TERMS - 1] = matrix_edge_ref[...]
    edge_out[TERMS - 1] = p_out[:, length - 1, :]


def lat_matrix(kappa_lat, sea_mask, kappa_lon):
    shape = kappa_lat.shape
    full = jax.ShapeDtypeStruct(shape, jnp.float32)
    edge = jax.ShapeDtypeStruct((TERMS - 2, shape[0], shape[2]), jnp.float32)
    return pl.pallas_call(
        lat_matrix_kernel,
        out_shape=(full, full, edge, full),
        scratch_shapes=[pltpu.VMEM(shape, jnp.float32)],
    )(kappa_lat, sea_mask, kappa_lon)


def lat_rhs(*inputs):
    shape = inputs[0].shape
    return pl.pallas_call(
        lat_rhs_kernel,
        out_shape=(
            jax.ShapeDtypeStruct(shape, jnp.float32),
            jax.ShapeDtypeStruct((TERMS, shape[0], shape[2]), jnp.float32),
        ),
    )(*inputs)


def circular_solve(lower_band, upper_band, excess, sources):
    devices = lower_band.shape[0]
    stride = 1
    while stride < devices:
        inverse = 1.0 / (excess - lower_band - upper_band)
        left_weight = -lower_band * jnp.roll(inverse, stride, 0)
        right_coefficient = -upper_band * jnp.roll(inverse, -stride, 0)
        new_lower = left_weight * jnp.roll(lower_band, stride, 0)
        new_upper = right_coefficient * jnp.roll(upper_band, -stride, 0)
        excess = (
            excess
            + left_weight * jnp.roll(excess, stride, 0)
            + right_coefficient * jnp.roll(excess, -stride, 0)
        )
        sources = (
            sources
            + left_weight * jnp.roll(sources, stride, 0)
            + right_coefficient * jnp.roll(sources, -stride, 0)
        )
        lower_band, upper_band = (new_lower, new_upper)
        stride = stride * 2
    return sources / excess


def flux_system(terms, periodic):
    head_p, head_u, head_w, tail_kappa, tail_u, tail_w, tail_p = terms
    devices = head_p.shape[0]

    def next_of(member):
        return jnp.roll(member, -1, 0)

    next_wet = jnp.where(next_of(head_u) > 0.0, 1.0, 0.0)
    face = tail_kappa * next_wet
    if not periodic:
        device = lax.broadcasted_iota(jnp.int32, face.shape, 0)
        face = jnp.where(device == devices - 1, 0.0, face)
        tail_kappa = jnp.where(device == devices - 1, 0.0, tail_kappa)
    lower = -face * tail_u
    upper = -tail_kappa * next_of(head_w)
    diagonal = 1.0 + tail_kappa * next_of(head_u) + face * tail_w
    return circular_solve(
        lower, upper, diagonal + lower + upper, tail_kappa * next_of(head_p) - face * tail_p
    )


def interface_flux(edge, axis, mesh_axis, periodic, exchange):
    terms = lax.slice_in_dim(edge, 0, TERMS, axis=axis) if edge.shape[axis] > TERMS else edge
    devices = lax.axis_size(mesh_axis)
    if exchange == "all_to_all":
        copies = jnp.broadcast_to(terms[None], (devices,) + terms.shape)
        gathered = lax.all_to_all(copies, mesh_axis, 0, 0, tiled=True)
    else:
        gathered = lax.all_gather(terms[None], mesh_axis, axis=0, tiled=True)
    terms = [lax.index_in_dim(gathered, k, axis + 1, keepdims=False) for k in range(TERMS)]
    flux = flux_system(terms, periodic)
    index = lax.axis_index(mesh_axis)
    here = lax.dynamic_index_in_dim(flux, index, 0, keepdims=True)
    before = lax.dynamic_index_in_dim(flux, (index + devices - 1) % devices, 0, keepdims=True)
    return before[0], here[0]


def lon_flux(copies):
    devices = copies.shape[0]
    gathered = lax.all_to_all(copies, "lon", 0, 0, tiled=True)
    terms = [gathered[:, k] for k in range(TERMS)]
    flux = flux_system(terms, True)
    index = lax.axis_index("lon")
    here = lax.dynamic_index_in_dim(flux, index, 0, keepdims=False)
    before = lax.dynamic_index_in_dim(flux, (index + devices - 1) % devices, 0, keepdims=False)
    return before, here


def shards(source, kappa_lon, kappa_lat, sea_mask):
    p_lon, u_lon, w_lon, edge_lon = lon_pass(source, kappa_lon, sea_mask, lax.axis_size("lon"))
    u_lat, w_lat, matrix_edge, scale = lat_matrix(kappa_lat, sea_mask, kappa_lon)
    before, here = lon_flux(edge_lon)
    flux = jnp.concatenate([before[None], here[None], jnp.zeros((6,) + before.shape, jnp.float32)], 0)
    p_lat, edge_lat = lat_rhs(
        p_lon, u_lon, w_lon, flux, kappa_lat, sea_mask, matrix_edge,
    )
    before, here = interface_flux(edge_lat, 0, "lat", False, "all_gather")
    return scale * (p_lat - u_lat * before[:, None, :] + w_lat * here[:, None, :])


def solution(mesh):
    return jax.shard_map(
        shards,
        mesh=mesh,
        in_specs=(
            P(None, "lat", "lon"),
            P(None, "lat", "lon"),
            P(None, "lat", "lon"),
            P(None, "lat", "lon"),
        ),
        out_specs=P(None, "lat", "lon"),
        check_vma=False,
    )
```

```python
import functools

import jax
import jax.numpy as jnp
from jax import lax
from jax.experimental import pallas as pl
from jax.experimental.pallas import tpu as pltpu
from jax.sharding import PartitionSpec as P

TERMS = 7


def shifted(values, shift, axis):
    length = values.shape[axis]
    return pltpu.roll(values, shift % length, axis)


def block_solve(lower_band, upper_band, excess, sources, axis, weights=None):
    length = lower_band.shape[axis]
    stride = 1
    while stride < length:
        inverse = 1.0 / (excess - lower_band - upper_band)
        left_weight = -lower_band * shifted(inverse, stride, axis)
        right_coefficient = -upper_band * shifted(inverse, -stride, axis)
        if weights is not None:
            weights.append((left_weight, right_coefficient))
        new_lower = left_weight * shifted(lower_band, stride, axis)
        new_upper = right_coefficient * shifted(upper_band, -stride, axis)
        excess = (
            excess
            + left_weight * shifted(excess, stride, axis)
            + right_coefficient * shifted(excess, -stride, axis)
        )
        sources = [
            member
            + left_weight * shifted(member, stride, axis)
            + right_coefficient * shifted(member, -stride, axis)
            for member in sources
        ]
        lower_band, upper_band = (new_lower, new_upper)
        stride = stride * 2
    diagonal = excess - lower_band - upper_band
    if weights is not None:
        weights.append(diagonal)
    return [member / diagonal for member in sources]


def pass_kernel(axis, corrected, *refs):
    if corrected:
        (p_ref, u_ref, w_ref, before_ref, here_ref, kappa_ref, mask_ref,
         p_out, u_out, w_out, edge_out) = refs
        values = (
            p_ref[...]
            - u_ref[...] * before_ref[...]
            + w_ref[...] * here_ref[...]
        )
    else:
        (source_ref, kappa_ref, mask_ref, p_out, u_out, w_out, edge_out) = refs
        values = source_ref[...]
    shape = values.shape
    length = shape[axis]
    wet = mask_ref[...].astype(jnp.float32)
    weight = kappa_ref[...].astype(jnp.float32) * wet
    position = lax.broadcasted_iota(jnp.int32, shape, axis)
    last = position == length - 1
    right_face = jnp.where(last, 0.0, weight * shifted(wet, -1, axis))
    left_face = shifted(right_face, 1, axis)
    first = position == 0
    particular, from_left, from_right = block_solve(
        -left_face,
        -right_face,
        jnp.ones(shape, jnp.float32),
        [values, jnp.where(first, 1.0, 0.0), jnp.where(last, 1.0, 0.0)],
        axis,
    )
    p_out[...] = particular
    u_out[...] = from_left
    w_out[...] = from_right
    tail_weight = shifted(weight, 4, axis)
    entries = [
        wet * particular,
        shifted(wet * from_left, 1, axis),
        shifted(wet * from_right, 2, axis),
        tail_weight,
        shifted(from_left, 4 + 1, axis),
        shifted(from_right, 4 + 2, axis),
        shifted(particular, 4 + 3, axis),
    ]
    edge = entries[0]
    for k in range(1, TERMS):
        edge = jnp.where(position == k, entries[k], edge)
    if axis == 2:
        edge_out[...] = edge
    else:
        edge_out[...] = lax.slice_in_dim(edge, 0, 8, axis=axis)


def local_pass(axis, inputs):
    shape = inputs[0].shape
    corrected = len(inputs) > 3
    edge_shape = shape if axis == 2 else shape[:axis] + (8,) + shape[axis + 1:]
    return pl.pallas_call(
        functools.partial(pass_kernel, axis, corrected),
        out_shape=(
            jax.ShapeDtypeStruct(shape, jnp.float32),
            jax.ShapeDtypeStruct(shape, jnp.float32),
            jax.ShapeDtypeStruct(shape, jnp.float32),
            jax.ShapeDtypeStruct(edge_shape, jnp.float32),
        ),
    )(*inputs)


def lon_kernel(source_ref, kappa_ref, mask_ref, p_out, u_out, w_out, edge_out):
    levels, rows, length = source_ref.shape
    lines = levels * rows

    def across(values):
        return jnp.transpose(values.astype(jnp.float32).reshape(lines, length))

    def back(values):
        return jnp.transpose(values).reshape(levels, rows, length)

    wet = across(mask_ref[...])
    weight = across(kappa_ref[...]) * wet
    values = across(source_ref[...])
    axis = 0
    shape = values.shape
    position = lax.broadcasted_iota(jnp.int32, shape, axis)
    last = position == length - 1
    right_face = jnp.where(last, 0.0, weight * shifted(wet, -1, axis))
    left_face = shifted(right_face, 1, axis)
    particular, from_left, from_right = block_solve(
        -left_face,
        -right_face,
        jnp.ones(shape, jnp.float32),
        [values, jnp.where(position == 0, 1.0, 0.0), jnp.where(last, 1.0, 0.0)],
        axis,
    )
    p_out[...] = back(particular)
    u_out[...] = back(from_left)
    w_out[...] = back(from_right)
    head_wet = wet[0:1, :]
    rows = [
        head_wet * particular[0:1, :],
        head_wet * from_left[0:1, :],
        head_wet * from_right[0:1, :],
        weight[length - 1:length, :],
        from_left[length - 1:length, :],
        from_right[length - 1:length, :],
        particular[length - 1:length, :],
    ]
    for copy in range(edge_out.shape[0]):
        for k, row in enumerate(rows):
            edge_out[copy, k:k + 1, :] = row


def lon_pass(source, kappa_lon, sea_mask, devices):
    shape = source.shape
    full = jax.ShapeDtypeStruct(shape, jnp.float32)
    edge = jax.ShapeDtypeStruct((devices, TERMS, shape[0] * shape[1]), jnp.float32)
    return pl.pallas_call(lon_kernel, out_shape=(full, full, full, edge))(source, kappa_lon, sea_mask)


def lat_matrix_kernel(kappa_ref, mask_ref, lon_kappa_ref, u_out, w_out, edge_out, scale_out,
                      weight_scratch):
    axis = 1
    wet, weight, position, left_face, right_face = lat_faces(kappa_ref, mask_ref, axis)
    lat_kappa = kappa_ref[...].astype(jnp.float32)
    scale_out[...] = wet * 4.0 * jnp.sqrt(jnp.sqrt(lon_kappa_ref[...].astype(jnp.float32) * lat_kappa))
    shape = wet.shape
    length = shape[axis]
    from_left, from_right = block_solve(
        -left_face,
        -right_face,
        jnp.ones(shape, jnp.float32),
        [jnp.where(position == 0, 1.0, 0.0), jnp.where(position == length - 1, 1.0, 0.0)],
        axis,
    )
    u_out[...] = from_left
    w_out[...] = from_right
    weight_scratch[...] = weight
    head_wet = mask_ref[:, 0, :].astype(jnp.float32)
    edge_out[0] = head_wet * u_out[:, 0, :]
    edge_out[1] = head_wet * w_out[:, 0, :]
    edge_out[2] = weight_scratch[:, length - 1, :]
    edge_out[3] = u_out[:, length - 1, :]
    edge_out[4] = w_out[:, length - 1, :]


def lat_faces(kappa_ref, mask_ref, axis):
    wet = mask_ref[...].astype(jnp.float32)
    weight = kappa_ref[...].astype(jnp.float32) * wet
    position = lax.broadcasted_iota(jnp.int32, wet.shape, axis)
    last = position == wet.shape[axis] - 1
    right_face = jnp.where(last, 0.0, weight * shifted(wet, -1, axis))
    left_face = shifted(right_face, 1, axis)
    return wet, weight, position, left_face, right_face


def lat_rhs_kernel(index_ref, gathered_ref, p_ref, u_ref, w_ref, kappa_ref, mask_ref,
                   matrix_edge_ref, p_out, edge_out):
    axis = 1
    terms = [gathered_ref[:, k, :] for k in range(TERMS)]
    flux = flux_system(terms, True, lambda values, shift, along: shifted(values, shift, along))
    devices, lines = flux.shape
    device = lax.broadcasted_iota(jnp.int32, flux.shape, 0)
    index = index_ref[0]

    def pick(place):
        return jnp.sum(jnp.where(device == place, flux, 0.0), axis=0, keepdims=True)

    levels, rows, width = p_ref.shape
    padded = jnp.concatenate(
        [
            pick((index + devices - 1) % devices),
            pick(index),
            jnp.zeros((width - 2, lines), jnp.float32),
        ],
        0,
    )
    columns = jnp.transpose(padded)
    before = columns[:, 0:1].reshape(levels, rows, 1)
    here = columns[:, 1:2].reshape(levels, rows, 1)
    values = p_ref[...] - u_ref[...] * before + w_ref[...] * here
    wet, weight, position, left_face, right_face = lat_faces(kappa_ref, mask_ref, axis)
    (particular,) = block_solve(
        -left_face, -right_face, jnp.ones(values.shape, jnp.float32), [values], axis
    )
    p_out[...] = particular
    length = values.shape[axis]
    edge_out[0] = mask_ref[:, 0, :].astype(jnp.float32) * p_out[:, 0, :]
    edge_out[1:TERMS - 1] = matrix_edge_ref[...]
    edge_out[TERMS - 1] = p_out[:, length - 1, :]


def lat_matrix(kappa_lat, sea_mask, kappa_lon):
    shape = kappa_lat.shape
    full = jax.ShapeDtypeStruct(shape, jnp.float32)
    edge = jax.ShapeDtypeStruct((TERMS - 2, shape[0], shape[2]), jnp.float32)
    return pl.pallas_call(
        lat_matrix_kernel,
        out_shape=(full, full, edge, full),
        scratch_shapes=[pltpu.VMEM(shape, jnp.float32)],
    )(kappa_lat, sea_mask, kappa_lon)


def lat_rhs(gathered, *inputs):
    shape = inputs[0].shape
    index = jnp.full((1,), lax.axis_index("lon"), jnp.int32)
    vmem = pl.BlockSpec(memory_space=pltpu.VMEM)
    return pl.pallas_call(
        lat_rhs_kernel,
        out_shape=(
            jax.ShapeDtypeStruct(shape, jnp.float32),
            jax.ShapeDtypeStruct((TERMS, shape[0], shape[2]), jnp.float32),
        ),
        in_specs=[pl.BlockSpec(memory_space=pltpu.SMEM)] + [vmem] * (1 + len(inputs)),
        out_specs=(vmem, vmem),
    )(index, gathered, *inputs)


def circular_solve(lower_band, upper_band, excess, sources, roll=jnp.roll):
    devices = lower_band.shape[0]
    stride = 1
    while stride < devices:
        inverse = 1.0 / (excess - lower_band - upper_band)
        left_weight = -lower_band * roll(inverse, stride, 0)
        right_coefficient = -upper_band * roll(inverse, -stride, 0)
        new_lower = left_weight * roll(lower_band, stride, 0)
        new_upper = right_coefficient * roll(upper_band, -stride, 0)
        excess = (
            excess
            + left_weight * roll(excess, stride, 0)
            + right_coefficient * roll(excess, -stride, 0)
        )
        sources = (
            sources
            + left_weight * roll(sources, stride, 0)
            + right_coefficient * roll(sources, -stride, 0)
        )
        lower_band, upper_band = (new_lower, new_upper)
        stride = stride * 2
    return sources / excess


def flux_system(terms, periodic, roll=jnp.roll):
    head_p, head_u, head_w, tail_kappa, tail_u, tail_w, tail_p = terms
    devices = head_p.shape[0]

    def next_of(member):
        return roll(member, -1, 0)

    next_wet = jnp.where(next_of(head_u) > 0.0, 1.0, 0.0)
    face = tail_kappa * next_wet
    if not periodic:
        device = lax.broadcasted_iota(jnp.int32, face.shape, 0)
        face = jnp.where(device == devices - 1, 0.0, face)
        tail_kappa = jnp.where(device == devices - 1, 0.0, tail_kappa)
    lower = -face * tail_u
    upper = -tail_kappa * next_of(head_w)
    diagonal = 1.0 + tail_kappa * next_of(head_u) + face * tail_w
    return circular_solve(
        lower, upper, diagonal + lower + upper, tail_kappa * next_of(head_p) - face * tail_p, roll
    )


def interface_flux(edge, axis, mesh_axis, periodic, exchange):
    terms = lax.slice_in_dim(edge, 0, TERMS, axis=axis) if edge.shape[axis] > TERMS else edge
    devices = lax.axis_size(mesh_axis)
    if exchange == "all_to_all":
        copies = jnp.broadcast_to(terms[None], (devices,) + terms.shape)
        gathered = lax.all_to_all(copies, mesh_axis, 0, 0, tiled=True)
    else:
        gathered = lax.all_gather(terms[None], mesh_axis, axis=0, tiled=True)
    terms = [lax.index_in_dim(gathered, k, axis + 1, keepdims=False) for k in range(TERMS)]
    flux = flux_system(terms, periodic)
    index = lax.axis_index(mesh_axis)
    here = lax.dynamic_index_in_dim(flux, index, 0, keepdims=True)
    before = lax.dynamic_index_in_dim(flux, (index + devices - 1) % devices, 0, keepdims=True)
    return before[0], here[0]


def lon_flux(copies):
    devices = copies.shape[0]
    gathered = lax.all_to_all(copies, "lon", 0, 0, tiled=True)
    terms = [gathered[:, k] for k in range(TERMS)]
    flux = flux_system(terms, True)
    index = lax.axis_index("lon")
    here = lax.dynamic_index_in_dim(flux, index, 0, keepdims=False)
    before = lax.dynamic_index_in_dim(flux, (index + devices - 1) % devices, 0, keepdims=False)
    return before, here


def shards(source, kappa_lon, kappa_lat, sea_mask):
    p_lon, u_lon, w_lon, edge_lon = lon_pass(source, kappa_lon, sea_mask, lax.axis_size("lon"))
    u_lat, w_lat, matrix_edge, scale = lat_matrix(kappa_lat, sea_mask, kappa_lon)
    gathered = lax.all_to_all(edge_lon, "lon", 0, 0, tiled=True)
    p_lat, edge_lat = lat_rhs(
        gathered, p_lon, u_lon, w_lon, kappa_lat, sea_mask, matrix_edge,
    )
    before, here = interface_flux(edge_lat, 0, "lat", False, "all_gather")
    return scale * (p_lat - u_lat * before[:, None, :] + w_lat * here[:, None, :])


def solution(mesh):
    return jax.shard_map(
        shards,
        mesh=mesh,
        in_specs=(
            P(None, "lat", "lon"),
            P(None, "lat", "lon"),
            P(None, "lat", "lon"),
            P(None, "lat", "lon"),
        ),
        out_specs=P(None, "lat", "lon"),
        check_vma=False,
    )
```

```python
import functools

import jax
import jax.numpy as jnp
from jax import lax
from jax.experimental import pallas as pl
from jax.experimental.pallas import tpu as pltpu
from jax.sharding import PartitionSpec as P

TERMS = 7


def shifted(values, shift, axis):
    length = values.shape[axis]
    return pltpu.roll(values, shift % length, axis)


def block_solve(lower_band, upper_band, excess, sources, axis, weights=None):
    length = lower_band.shape[axis]
    stride = 1
    while stride < length:
        inverse = 1.0 / (excess - lower_band - upper_band)
        left_weight = -lower_band * shifted(inverse, stride, axis)
        right_coefficient = -upper_band * shifted(inverse, -stride, axis)
        if weights is not None:
            weights.append((left_weight, right_coefficient))
        new_lower = left_weight * shifted(lower_band, stride, axis)
        new_upper = right_coefficient * shifted(upper_band, -stride, axis)
        excess = (
            excess
            + left_weight * shifted(excess, stride, axis)
            + right_coefficient * shifted(excess, -stride, axis)
        )
        sources = [
            member
            + left_weight * shifted(member, stride, axis)
            + right_coefficient * shifted(member, -stride, axis)
            for member in sources
        ]
        lower_band, upper_band = (new_lower, new_upper)
        stride = stride * 2
    diagonal = excess - lower_band - upper_band
    if weights is not None:
        weights.append(diagonal)
    return [member / diagonal for member in sources]


def pass_kernel(axis, corrected, *refs):
    if corrected:
        (p_ref, u_ref, w_ref, before_ref, here_ref, kappa_ref, mask_ref,
         p_out, u_out, w_out, edge_out) = refs
        values = (
            p_ref[...]
            - u_ref[...] * before_ref[...]
            + w_ref[...] * here_ref[...]
        )
    else:
        (source_ref, kappa_ref, mask_ref, p_out, u_out, w_out, edge_out) = refs
        values = source_ref[...]
    shape = values.shape
    length = shape[axis]
    wet = mask_ref[...].astype(jnp.float32)
    weight = kappa_ref[...].astype(jnp.float32) * wet
    position = lax.broadcasted_iota(jnp.int32, shape, axis)
    last = position == length - 1
    right_face = jnp.where(last, 0.0, weight * shifted(wet, -1, axis))
    left_face = shifted(right_face, 1, axis)
    first = position == 0
    particular, from_left, from_right = block_solve(
        -left_face,
        -right_face,
        jnp.ones(shape, jnp.float32),
        [values, jnp.where(first, 1.0, 0.0), jnp.where(last, 1.0, 0.0)],
        axis,
    )
    p_out[...] = particular
    u_out[...] = from_left
    w_out[...] = from_right
    tail_weight = shifted(weight, 4, axis)
    entries = [
        wet * particular,
        shifted(wet * from_left, 1, axis),
        shifted(wet * from_right, 2, axis),
        tail_weight,
        shifted(from_left, 4 + 1, axis),
        shifted(from_right, 4 + 2, axis),
        shifted(particular, 4 + 3, axis),
    ]
    edge = entries[0]
    for k in range(1, TERMS):
        edge = jnp.where(position == k, entries[k], edge)
    if axis == 2:
        edge_out[...] = edge
    else:
        edge_out[...] = lax.slice_in_dim(edge, 0, 8, axis=axis)


def local_pass(axis, inputs):
    shape = inputs[0].shape
    corrected = len(inputs) > 3
    edge_shape = shape if axis == 2 else shape[:axis] + (8,) + shape[axis + 1:]
    return pl.pallas_call(
        functools.partial(pass_kernel, axis, corrected),
        out_shape=(
            jax.ShapeDtypeStruct(shape, jnp.float32),
            jax.ShapeDtypeStruct(shape, jnp.float32),
            jax.ShapeDtypeStruct(shape, jnp.float32),
            jax.ShapeDtypeStruct(edge_shape, jnp.float32),
        ),
    )(*inputs)


def lon_kernel(source_ref, kappa_ref, mask_ref, p_out, u_out, w_out, edge_out):
    levels, rows, length = source_ref.shape
    lines = levels * rows

    def across(values):
        return jnp.transpose(values.astype(jnp.float32).reshape(lines, length))

    def back(values):
        return jnp.transpose(values).reshape(levels, rows, length)

    wet = across(mask_ref[...])
    weight = across(kappa_ref[...]) * wet
    values = across(source_ref[...])
    axis = 0
    shape = values.shape
    position = lax.broadcasted_iota(jnp.int32, shape, axis)
    last = position == length - 1
    right_face = jnp.where(last, 0.0, weight * shifted(wet, -1, axis))
    left_face = shifted(right_face, 1, axis)
    particular, from_left, from_right = block_solve(
        -left_face,
        -right_face,
        jnp.ones(shape, jnp.float32),
        [values, jnp.where(position == 0, 1.0, 0.0), jnp.where(last, 1.0, 0.0)],
        axis,
    )
    p_out[...] = back(particular)
    u_out[...] = back(from_left)
    w_out[...] = back(from_right)
    head_wet = wet[0:1, :]
    rows = [
        head_wet * particular[0:1, :],
        head_wet * from_left[0:1, :],
        head_wet * from_right[0:1, :],
        weight[length - 1:length, :],
        from_left[length - 1:length, :],
        from_right[length - 1:length, :],
        particular[length - 1:length, :],
    ]
    for copy in range(edge_out.shape[0]):
        for k, row in enumerate(rows):
            edge_out[copy, k:k + 1, :] = row


def lon_pass(source, kappa_lon, sea_mask, devices):
    shape = source.shape
    full = jax.ShapeDtypeStruct(shape, jnp.float32)
    edge = jax.ShapeDtypeStruct((devices, TERMS, shape[0] * shape[1]), jnp.float32)
    return pl.pallas_call(lon_kernel, out_shape=(full, full, full, edge))(source, kappa_lon, sea_mask)


def lat_matrix_kernel(kappa_ref, mask_ref, lon_kappa_ref, u_out, w_out, edge_out, scale_out,
                      weight_scratch):
    axis = 1
    wet, weight, position, left_face, right_face = lat_faces(kappa_ref, mask_ref, axis)
    lat_kappa = kappa_ref[...].astype(jnp.float32)
    scale_out[...] = wet * 4.0 * jnp.sqrt(jnp.sqrt(lon_kappa_ref[...].astype(jnp.float32) * lat_kappa))
    shape = wet.shape
    length = shape[axis]
    from_left, from_right = block_solve(
        -left_face,
        -right_face,
        jnp.ones(shape, jnp.float32),
        [jnp.where(position == 0, 1.0, 0.0), jnp.where(position == length - 1, 1.0, 0.0)],
        axis,
    )
    u_out[...] = from_left
    w_out[...] = from_right
    weight_scratch[...] = weight
    head_wet = mask_ref[:, 0, :].astype(jnp.float32)
    edge_out[0] = head_wet * u_out[:, 0, :]
    edge_out[1] = head_wet * w_out[:, 0, :]
    edge_out[2] = weight_scratch[:, length - 1, :]
    edge_out[3] = u_out[:, length - 1, :]
    edge_out[4] = w_out[:, length - 1, :]
    u_out[...] = scale_out[...] * from_left
    w_out[...] = scale_out[...] * from_right


def lat_faces(kappa_ref, mask_ref, axis):
    wet = mask_ref[...].astype(jnp.float32)
    weight = kappa_ref[...].astype(jnp.float32) * wet
    position = lax.broadcasted_iota(jnp.int32, wet.shape, axis)
    last = position == wet.shape[axis] - 1
    right_face = jnp.where(last, 0.0, weight * shifted(wet, -1, axis))
    left_face = shifted(right_face, 1, axis)
    return wet, weight, position, left_face, right_face


def lat_rhs_kernel(index_ref, gathered_ref, p_ref, u_ref, w_ref, kappa_ref, mask_ref,
                   matrix_edge_ref, scale_ref, p_out, edge_out):
    axis = 1
    terms = [gathered_ref[:, k, :] for k in range(TERMS)]
    flux = flux_system(terms, True, lambda values, shift, along: shifted(values, shift, along))
    devices, lines = flux.shape
    device = lax.broadcasted_iota(jnp.int32, flux.shape, 0)
    index = index_ref[0]

    def pick(place):
        return jnp.sum(jnp.where(device == place, flux, 0.0), axis=0, keepdims=True)

    levels, rows, width = p_ref.shape
    padded = jnp.concatenate(
        [
            pick((index + devices - 1) % devices),
            pick(index),
            jnp.zeros((width - 2, lines), jnp.float32),
        ],
        0,
    )
    columns = jnp.transpose(padded)
    before = columns[:, 0:1].reshape(levels, rows, 1)
    here = columns[:, 1:2].reshape(levels, rows, 1)
    values = p_ref[...] - u_ref[...] * before + w_ref[...] * here
    wet, weight, position, left_face, right_face = lat_faces(kappa_ref, mask_ref, axis)
    (particular,) = block_solve(
        -left_face, -right_face, jnp.ones(values.shape, jnp.float32), [values], axis
    )
    p_out[...] = particular
    length = values.shape[axis]
    edge_out[0] = mask_ref[:, 0, :].astype(jnp.float32) * p_out[:, 0, :]
    edge_out[1:TERMS - 1] = matrix_edge_ref[...]
    edge_out[TERMS - 1] = p_out[:, length - 1, :]
    p_out[...] = scale_ref[...] * particular


def lat_matrix(kappa_lat, sea_mask, kappa_lon):
    shape = kappa_lat.shape
    full = jax.ShapeDtypeStruct(shape, jnp.float32)
    edge = jax.ShapeDtypeStruct((TERMS - 2, shape[0], shape[2]), jnp.float32)
    return pl.pallas_call(
        lat_matrix_kernel,
        out_shape=(full, full, edge, full),
        scratch_shapes=[pltpu.VMEM(shape, jnp.float32)],
    )(kappa_lat, sea_mask, kappa_lon)


def lat_rhs(gathered, *inputs):
    shape = inputs[0].shape
    index = jnp.full((1,), lax.axis_index("lon"), jnp.int32)
    vmem = pl.BlockSpec(memory_space=pltpu.VMEM)
    return pl.pallas_call(
        lat_rhs_kernel,
        out_shape=(
            jax.ShapeDtypeStruct(shape, jnp.float32),
            jax.ShapeDtypeStruct((TERMS, shape[0], shape[2]), jnp.float32),
        ),
        in_specs=[pl.BlockSpec(memory_space=pltpu.SMEM)] + [vmem] * (1 + len(inputs)),
        out_specs=(vmem, vmem),
    )(index, gathered, *inputs)


def circular_solve(lower_band, upper_band, excess, sources, roll=jnp.roll):
    devices = lower_band.shape[0]
    stride = 1
    while stride < devices:
        inverse = 1.0 / (excess - lower_band - upper_band)
        left_weight = -lower_band * roll(inverse, stride, 0)
        right_coefficient = -upper_band * roll(inverse, -stride, 0)
        new_lower = left_weight * roll(lower_band, stride, 0)
        new_upper = right_coefficient * roll(upper_band, -stride, 0)
        excess = (
            excess
            + left_weight * roll(excess, stride, 0)
            + right_coefficient * roll(excess, -stride, 0)
        )
        sources = (
            sources
            + left_weight * roll(sources, stride, 0)
            + right_coefficient * roll(sources, -stride, 0)
        )
        lower_band, upper_band = (new_lower, new_upper)
        stride = stride * 2
    return sources / excess


def flux_system(terms, periodic, roll=jnp.roll):
    head_p, head_u, head_w, tail_kappa, tail_u, tail_w, tail_p = terms
    devices = head_p.shape[0]

    def next_of(member):
        return roll(member, -1, 0)

    next_wet = jnp.where(next_of(head_u) > 0.0, 1.0, 0.0)
    face = tail_kappa * next_wet
    if not periodic:
        device = lax.broadcasted_iota(jnp.int32, face.shape, 0)
        face = jnp.where(device == devices - 1, 0.0, face)
        tail_kappa = jnp.where(device == devices - 1, 0.0, tail_kappa)
    lower = -face * tail_u
    upper = -tail_kappa * next_of(head_w)
    diagonal = 1.0 + tail_kappa * next_of(head_u) + face * tail_w
    return circular_solve(
        lower, upper, diagonal + lower + upper, tail_kappa * next_of(head_p) - face * tail_p, roll
    )


def interface_flux(edge, axis, mesh_axis, periodic, exchange):
    terms = lax.slice_in_dim(edge, 0, TERMS, axis=axis) if edge.shape[axis] > TERMS else edge
    devices = lax.axis_size(mesh_axis)
    if exchange == "all_to_all":
        copies = jnp.broadcast_to(terms[None], (devices,) + terms.shape)
        gathered = lax.all_to_all(copies, mesh_axis, 0, 0, tiled=True)
    else:
        gathered = lax.all_gather(terms[None], mesh_axis, axis=0, tiled=True)
    terms = [lax.index_in_dim(gathered, k, axis + 1, keepdims=False) for k in range(TERMS)]
    flux = flux_system(terms, periodic)
    index = lax.axis_index(mesh_axis)
    here = lax.dynamic_index_in_dim(flux, index, 0, keepdims=True)
    before = lax.dynamic_index_in_dim(flux, (index + devices - 1) % devices, 0, keepdims=True)
    return before[0], here[0]


def lon_flux(copies):
    devices = copies.shape[0]
    gathered = lax.all_to_all(copies, "lon", 0, 0, tiled=True)
    terms = [gathered[:, k] for k in range(TERMS)]
    flux = flux_system(terms, True)
    index = lax.axis_index("lon")
    here = lax.dynamic_index_in_dim(flux, index, 0, keepdims=False)
    before = lax.dynamic_index_in_dim(flux, (index + devices - 1) % devices, 0, keepdims=False)
    return before, here


def shards(source, kappa_lon, kappa_lat, sea_mask):
    p_lon, u_lon, w_lon, edge_lon = lon_pass(source, kappa_lon, sea_mask, lax.axis_size("lon"))
    u_lat, w_lat, matrix_edge, scale = lat_matrix(kappa_lat, sea_mask, kappa_lon)
    gathered = lax.all_to_all(edge_lon, "lon", 0, 0, tiled=True)
    p_lat, edge_lat = lat_rhs(
        gathered, p_lon, u_lon, w_lon, kappa_lat, sea_mask, matrix_edge, scale,
    )
    before, here = interface_flux(edge_lat, 0, "lat", False, "all_gather")
    return p_lat - u_lat * before[:, None, :] + w_lat * here[:, None, :]


def solution(mesh):
    return jax.shard_map(
        shards,
        mesh=mesh,
        in_specs=(
            P(None, "lat", "lon"),
            P(None, "lat", "lon"),
            P(None, "lat", "lon"),
            P(None, "lat", "lon"),
        ),
        out_specs=P(None, "lat", "lon"),
        check_vma=False,
    )
```

```python
import functools

import jax
import jax.numpy as jnp
from jax import lax
from jax.experimental import pallas as pl
from jax.experimental.pallas import tpu as pltpu
from jax.sharding import PartitionSpec as P

TERMS = 7


def shifted(values, shift, axis):
    length = values.shape[axis]
    return pltpu.roll(values, shift % length, axis)


def block_solve(lower_band, upper_band, excess, sources, axis, weights=None):
    length = lower_band.shape[axis]
    stride = 1
    while stride < length:
        inverse = 1.0 / (excess - lower_band - upper_band)
        left_weight = -lower_band * shifted(inverse, stride, axis)
        right_coefficient = -upper_band * shifted(inverse, -stride, axis)
        if weights is not None:
            weights.append((left_weight, right_coefficient))
        new_lower = left_weight * shifted(lower_band, stride, axis)
        new_upper = right_coefficient * shifted(upper_band, -stride, axis)
        excess = (
            excess
            + left_weight * shifted(excess, stride, axis)
            + right_coefficient * shifted(excess, -stride, axis)
        )
        sources = [
            member
            + left_weight * shifted(member, stride, axis)
            + right_coefficient * shifted(member, -stride, axis)
            for member in sources
        ]
        lower_band, upper_band = (new_lower, new_upper)
        stride = stride * 2
    diagonal = excess - lower_band - upper_band
    if weights is not None:
        weights.append(diagonal)
    return [member / diagonal for member in sources]


def pass_kernel(axis, corrected, *refs):
    if corrected:
        (p_ref, u_ref, w_ref, before_ref, here_ref, kappa_ref, mask_ref,
         p_out, u_out, w_out, edge_out) = refs
        values = (
            p_ref[...]
            - u_ref[...] * before_ref[...]
            + w_ref[...] * here_ref[...]
        )
    else:
        (source_ref, kappa_ref, mask_ref, p_out, u_out, w_out, edge_out) = refs
        values = source_ref[...]
    shape = values.shape
    length = shape[axis]
    wet = mask_ref[...].astype(jnp.float32)
    weight = kappa_ref[...].astype(jnp.float32) * wet
    position = lax.broadcasted_iota(jnp.int32, shape, axis)
    last = position == length - 1
    right_face = jnp.where(last, 0.0, weight * shifted(wet, -1, axis))
    left_face = shifted(right_face, 1, axis)
    first = position == 0
    particular, from_left, from_right = block_solve(
        -left_face,
        -right_face,
        jnp.ones(shape, jnp.float32),
        [values, jnp.where(first, 1.0, 0.0), jnp.where(last, 1.0, 0.0)],
        axis,
    )
    p_out[...] = particular
    u_out[...] = from_left
    w_out[...] = from_right
    tail_weight = shifted(weight, 4, axis)
    entries = [
        wet * particular,
        shifted(wet * from_left, 1, axis),
        shifted(wet * from_right, 2, axis),
        tail_weight,
        shifted(from_left, 4 + 1, axis),
        shifted(from_right, 4 + 2, axis),
        shifted(particular, 4 + 3, axis),
    ]
    edge = entries[0]
    for k in range(1, TERMS):
        edge = jnp.where(position == k, entries[k], edge)
    if axis == 2:
        edge_out[...] = edge
    else:
        edge_out[...] = lax.slice_in_dim(edge, 0, 8, axis=axis)


def local_pass(axis, inputs):
    shape = inputs[0].shape
    corrected = len(inputs) > 3
    edge_shape = shape if axis == 2 else shape[:axis] + (8,) + shape[axis + 1:]
    return pl.pallas_call(
        functools.partial(pass_kernel, axis, corrected),
        out_shape=(
            jax.ShapeDtypeStruct(shape, jnp.float32),
            jax.ShapeDtypeStruct(shape, jnp.float32),
            jax.ShapeDtypeStruct(shape, jnp.float32),
            jax.ShapeDtypeStruct(edge_shape, jnp.float32),
        ),
    )(*inputs)


def lon_kernel(source_ref, kappa_ref, mask_ref, p_out, u_out, w_out, edge_out):
    levels, rows, length = source_ref.shape
    lines = levels * rows

    def across(values):
        return jnp.transpose(values.astype(jnp.float32).reshape(lines, length))

    def back(values):
        return jnp.transpose(values).reshape(levels, rows, length)

    wet = across(mask_ref[...])
    weight = across(kappa_ref[...]) * wet
    values = across(source_ref[...])
    axis = 0
    shape = values.shape
    position = lax.broadcasted_iota(jnp.int32, shape, axis)
    last = position == length - 1
    right_face = jnp.where(last, 0.0, weight * shifted(wet, -1, axis))
    left_face = shifted(right_face, 1, axis)
    particular, from_left, from_right = block_solve(
        -left_face,
        -right_face,
        jnp.ones(shape, jnp.float32),
        [values, jnp.where(position == 0, 1.0, 0.0), jnp.where(last, 1.0, 0.0)],
        axis,
    )
    p_out[...] = back(particular)
    u_out[...] = back(from_left)
    w_out[...] = back(from_right)
    head_wet = wet[0:1, :]
    rows = [
        head_wet * particular[0:1, :],
        head_wet * from_left[0:1, :],
        head_wet * from_right[0:1, :],
        weight[length - 1:length, :],
        from_left[length - 1:length, :],
        from_right[length - 1:length, :],
        particular[length - 1:length, :],
    ]
    for copy in range(edge_out.shape[0]):
        for k, row in enumerate(rows):
            edge_out[copy, k:k + 1, :] = row


def lon_pass(source, kappa_lon, sea_mask, devices):
    shape = source.shape
    full = jax.ShapeDtypeStruct(shape, jnp.float32)
    edge = jax.ShapeDtypeStruct((devices, TERMS, shape[0] * shape[1]), jnp.float32)
    return pl.pallas_call(lon_kernel, out_shape=(full, full, full, edge))(source, kappa_lon, sea_mask)


def lat_matrix_kernel(kappa_ref, mask_ref, lon_kappa_ref, u_out, w_out, edge_out, scale_out,
                      weight_scratch):
    axis = 1
    wet, weight, position, left_face, right_face = lat_faces(kappa_ref, mask_ref, axis)
    lat_kappa = kappa_ref[...].astype(jnp.float32)
    scale_out[...] = wet * 4.0 * jnp.sqrt(jnp.sqrt(lon_kappa_ref[...].astype(jnp.float32) * lat_kappa))
    shape = wet.shape
    length = shape[axis]
    from_left, from_right = block_solve(
        -left_face,
        -right_face,
        jnp.ones(shape, jnp.float32),
        [jnp.where(position == 0, 1.0, 0.0), jnp.where(position == length - 1, 1.0, 0.0)],
        axis,
    )
    u_out[...] = from_left
    w_out[...] = from_right
    weight_scratch[...] = weight
    head_wet = mask_ref[:, 0, :].astype(jnp.float32)
    edge_out[0] = head_wet * u_out[:, 0, :]
    edge_out[1] = head_wet * w_out[:, 0, :]
    edge_out[2] = weight_scratch[:, length - 1, :]
    edge_out[3] = u_out[:, length - 1, :]
    edge_out[4] = w_out[:, length - 1, :]


def lat_faces(kappa_ref, mask_ref, axis):
    wet = mask_ref[...].astype(jnp.float32)
    weight = kappa_ref[...].astype(jnp.float32) * wet
    position = lax.broadcasted_iota(jnp.int32, wet.shape, axis)
    last = position == wet.shape[axis] - 1
    right_face = jnp.where(last, 0.0, weight * shifted(wet, -1, axis))
    left_face = shifted(right_face, 1, axis)
    return wet, weight, position, left_face, right_face


def lat_rhs_kernel(index_ref, gathered_ref, p_ref, u_ref, w_ref, kappa_ref, mask_ref,
                   matrix_edge_ref, p_out, edge_out):
    axis = 1
    terms = [gathered_ref[:, k, :] for k in range(TERMS)]
    flux = flux_system(terms, True, lambda values, shift, along: shifted(values, shift, along))
    devices, lines = flux.shape
    device = lax.broadcasted_iota(jnp.int32, flux.shape, 0)
    index = index_ref[0]

    def pick(place):
        return jnp.sum(jnp.where(device == place, flux, 0.0), axis=0, keepdims=True)

    levels, rows, width = p_ref.shape
    padded = jnp.concatenate(
        [
            pick((index + devices - 1) % devices),
            pick(index),
            jnp.zeros((width - 2, lines), jnp.float32),
        ],
        0,
    )
    columns = jnp.transpose(padded)
    before = columns[:, 0:1].reshape(levels, rows, 1)
    here = columns[:, 1:2].reshape(levels, rows, 1)
    values = p_ref[...] - u_ref[...] * before + w_ref[...] * here
    wet, weight, position, left_face, right_face = lat_faces(kappa_ref, mask_ref, axis)
    (particular,) = block_solve(
        -left_face, -right_face, jnp.ones(values.shape, jnp.float32), [values], axis
    )
    p_out[...] = particular
    length = values.shape[axis]
    edge_out[0] = mask_ref[:, 0, :].astype(jnp.float32) * p_out[:, 0, :]
    edge_out[1:TERMS - 1] = matrix_edge_ref[...]
    edge_out[TERMS - 1] = p_out[:, length - 1, :]


def lat_matrix(kappa_lat, sea_mask, kappa_lon):
    shape = kappa_lat.shape
    full = jax.ShapeDtypeStruct(shape, jnp.float32)
    edge = jax.ShapeDtypeStruct((TERMS - 2, shape[0], shape[2]), jnp.float32)
    return pl.pallas_call(
        lat_matrix_kernel,
        out_shape=(full, full, edge, full),
        scratch_shapes=[pltpu.VMEM(shape, jnp.float32)],
    )(kappa_lat, sea_mask, kappa_lon)


def lat_rhs(gathered, *inputs):
    shape = inputs[0].shape
    index = jnp.full((1,), lax.axis_index("lon"), jnp.int32)
    vmem = pl.BlockSpec(memory_space=pltpu.VMEM)
    return pl.pallas_call(
        lat_rhs_kernel,
        out_shape=(
            jax.ShapeDtypeStruct(shape, jnp.float32),
            jax.ShapeDtypeStruct((TERMS, shape[0], shape[2]), jnp.float32),
        ),
        in_specs=[pl.BlockSpec(memory_space=pltpu.SMEM)] + [vmem] * (1 + len(inputs)),
        out_specs=(vmem, vmem),
    )(index, gathered, *inputs)


def circular_solve(lower_band, upper_band, excess, sources, roll=jnp.roll):
    devices = lower_band.shape[0]
    stride = 1
    while stride < devices:
        inverse = 1.0 / (excess - lower_band - upper_band)
        left_weight = -lower_band * roll(inverse, stride, 0)
        right_coefficient = -upper_band * roll(inverse, -stride, 0)
        new_lower = left_weight * roll(lower_band, stride, 0)
        new_upper = right_coefficient * roll(upper_band, -stride, 0)
        excess = (
            excess
            + left_weight * roll(excess, stride, 0)
            + right_coefficient * roll(excess, -stride, 0)
        )
        sources = (
            sources
            + left_weight * roll(sources, stride, 0)
            + right_coefficient * roll(sources, -stride, 0)
        )
        lower_band, upper_band = (new_lower, new_upper)
        stride = stride * 2
    return sources / excess


def flux_system(terms, periodic, roll=jnp.roll):
    head_p, head_u, head_w, tail_kappa, tail_u, tail_w, tail_p = terms
    devices = head_p.shape[0]

    def next_of(member):
        return roll(member, -1, 0)

    next_wet = jnp.where(next_of(head_u) > 0.0, 1.0, 0.0)
    face = tail_kappa * next_wet
    if not periodic:
        device = lax.broadcasted_iota(jnp.int32, face.shape, 0)
        face = jnp.where(device == devices - 1, 0.0, face)
        tail_kappa = jnp.where(device == devices - 1, 0.0, tail_kappa)
    lower = -face * tail_u
    upper = -tail_kappa * next_of(head_w)
    diagonal = 1.0 + tail_kappa * next_of(head_u) + face * tail_w
    if not periodic:
        sources = tail_kappa * next_of(head_p) - face * tail_p
        ratios, reduced = [], []
        for place in range(devices):
            pivot = diagonal[place]
            source = sources[place]
            if place > 0:
                pivot = pivot - lower[place] * ratios[-1]
                source = source - lower[place] * reduced[-1]
            ratios.append(upper[place] / pivot)
            reduced.append(source / pivot)
        solved = [reduced[-1]]
        for place in range(devices - 2, -1, -1):
            solved.append(reduced[place] - ratios[place] * solved[-1])
        return jnp.stack(solved[::-1], 0)
    return circular_solve(
        lower, upper, diagonal + lower + upper, tail_kappa * next_of(head_p) - face * tail_p, roll
    )


def interface_flux(edge, axis, mesh_axis, periodic, exchange):
    terms = lax.slice_in_dim(edge, 0, TERMS, axis=axis) if edge.shape[axis] > TERMS else edge
    devices = lax.axis_size(mesh_axis)
    if exchange == "all_to_all":
        copies = jnp.broadcast_to(terms[None], (devices,) + terms.shape)
        gathered = lax.all_to_all(copies, mesh_axis, 0, 0, tiled=True)
    else:
        gathered = lax.all_gather(terms[None], mesh_axis, axis=0, tiled=True)
    terms = [lax.index_in_dim(gathered, k, axis + 1, keepdims=False) for k in range(TERMS)]
    flux = flux_system(terms, periodic)
    index = lax.axis_index(mesh_axis)
    here = lax.dynamic_index_in_dim(flux, index, 0, keepdims=True)
    before = lax.dynamic_index_in_dim(flux, (index + devices - 1) % devices, 0, keepdims=True)
    return before[0], here[0]


def lon_flux(copies):
    devices = copies.shape[0]
    gathered = lax.all_to_all(copies, "lon", 0, 0, tiled=True)
    terms = [gathered[:, k] for k in range(TERMS)]
    flux = flux_system(terms, True)
    index = lax.axis_index("lon")
    here = lax.dynamic_index_in_dim(flux, index, 0, keepdims=False)
    before = lax.dynamic_index_in_dim(flux, (index + devices - 1) % devices, 0, keepdims=False)
    return before, here


def shards(source, kappa_lon, kappa_lat, sea_mask):
    p_lon, u_lon, w_lon, edge_lon = lon_pass(source, kappa_lon, sea_mask, lax.axis_size("lon"))
    u_lat, w_lat, matrix_edge, scale = lat_matrix(kappa_lat, sea_mask, kappa_lon)
    gathered = lax.all_to_all(edge_lon, "lon", 0, 0, tiled=True)
    p_lat, edge_lat = lat_rhs(
        gathered, p_lon, u_lon, w_lon, kappa_lat, sea_mask, matrix_edge,
    )
    before, here = interface_flux(edge_lat, 0, "lat", False, "all_gather")
    return scale * (p_lat - u_lat * before[:, None, :] + w_lat * here[:, None, :])


def solution(mesh):
    return jax.shard_map(
        shards,
        mesh=mesh,
        in_specs=(
            P(None, "lat", "lon"),
            P(None, "lat", "lon"),
            P(None, "lat", "lon"),
            P(None, "lat", "lon"),
        ),
        out_specs=P(None, "lat", "lon"),
        check_vma=False,
    )
```

```python
import functools

import jax
import jax.numpy as jnp
from jax import lax
from jax.experimental import pallas as pl
from jax.experimental.pallas import tpu as pltpu
from jax.sharding import PartitionSpec as P

TERMS = 7


def shifted(values, shift, axis):
    length = values.shape[axis]
    return pltpu.roll(values, shift % length, axis)


def block_solve(lower_band, upper_band, excess, sources, axis, weights=None):
    length = lower_band.shape[axis]
    stride = 1
    while stride < length:
        inverse = 1.0 / (excess - lower_band - upper_band)
        left_weight = -lower_band * shifted(inverse, stride, axis)
        right_coefficient = -upper_band * shifted(inverse, -stride, axis)
        if weights is not None:
            weights.append((left_weight, right_coefficient))
        new_lower = left_weight * shifted(lower_band, stride, axis)
        new_upper = right_coefficient * shifted(upper_band, -stride, axis)
        excess = (
            excess
            + left_weight * shifted(excess, stride, axis)
            + right_coefficient * shifted(excess, -stride, axis)
        )
        sources = [
            member
            + left_weight * shifted(member, stride, axis)
            + right_coefficient * shifted(member, -stride, axis)
            for member in sources
        ]
        lower_band, upper_band = (new_lower, new_upper)
        stride = stride * 2
    diagonal = excess - lower_band - upper_band
    if weights is not None:
        weights.append(diagonal)
    if len(sources) == 1:
        return [sources[0] / diagonal]
    inverse = 1.0 / diagonal
    return [member * inverse for member in sources]


def pass_kernel(axis, corrected, *refs):
    if corrected:
        (p_ref, u_ref, w_ref, before_ref, here_ref, kappa_ref, mask_ref,
         p_out, u_out, w_out, edge_out) = refs
        values = (
            p_ref[...]
            - u_ref[...] * before_ref[...]
            + w_ref[...] * here_ref[...]
        )
    else:
        (source_ref, kappa_ref, mask_ref, p_out, u_out, w_out, edge_out) = refs
        values = source_ref[...]
    shape = values.shape
    length = shape[axis]
    wet = mask_ref[...].astype(jnp.float32)
    weight = kappa_ref[...].astype(jnp.float32) * wet
    position = lax.broadcasted_iota(jnp.int32, shape, axis)
    last = position == length - 1
    right_face = jnp.where(last, 0.0, weight * shifted(wet, -1, axis))
    left_face = shifted(right_face, 1, axis)
    first = position == 0
    particular, from_left, from_right = block_solve(
        -left_face,
        -right_face,
        jnp.ones(shape, jnp.float32),
        [values, jnp.where(first, 1.0, 0.0), jnp.where(last, 1.0, 0.0)],
        axis,
    )
    p_out[...] = particular
    u_out[...] = from_left
    w_out[...] = from_right
    tail_weight = shifted(weight, 4, axis)
    entries = [
        wet * particular,
        shifted(wet * from_left, 1, axis),
        shifted(wet * from_right, 2, axis),
        tail_weight,
        shifted(from_left, 4 + 1, axis),
        shifted(from_right, 4 + 2, axis),
        shifted(particular, 4 + 3, axis),
    ]
    edge = entries[0]
    for k in range(1, TERMS):
        edge = jnp.where(position == k, entries[k], edge)
    if axis == 2:
        edge_out[...] = edge
    else:
        edge_out[...] = lax.slice_in_dim(edge, 0, 8, axis=axis)


def local_pass(axis, inputs):
    shape = inputs[0].shape
    corrected = len(inputs) > 3
    edge_shape = shape if axis == 2 else shape[:axis] + (8,) + shape[axis + 1:]
    return pl.pallas_call(
        functools.partial(pass_kernel, axis, corrected),
        out_shape=(
            jax.ShapeDtypeStruct(shape, jnp.float32),
            jax.ShapeDtypeStruct(shape, jnp.float32),
            jax.ShapeDtypeStruct(shape, jnp.float32),
            jax.ShapeDtypeStruct(edge_shape, jnp.float32),
        ),
    )(*inputs)


def lon_kernel(source_ref, kappa_ref, mask_ref, p_out, u_out, w_out, edge_out):
    levels, rows, length = source_ref.shape
    lines = levels * rows

    def across(values):
        return jnp.transpose(values.astype(jnp.float32).reshape(lines, length))

    def back(values):
        return jnp.transpose(values).reshape(levels, rows, length)

    wet = across(mask_ref[...])
    weight = across(kappa_ref[...]) * wet
    values = across(source_ref[...])
    axis = 0
    shape = values.shape
    position = lax.broadcasted_iota(jnp.int32, shape, axis)
    last = position == length - 1
    right_face = jnp.where(last, 0.0, weight * shifted(wet, -1, axis))
    left_face = shifted(right_face, 1, axis)
    particular, from_left, from_right = block_solve(
        -left_face,
        -right_face,
        jnp.ones(shape, jnp.float32),
        [values, jnp.where(position == 0, 1.0, 0.0), jnp.where(last, 1.0, 0.0)],
        axis,
    )
    p_out[...] = back(particular)
    u_out[...] = back(from_left)
    w_out[...] = back(from_right)
    head_wet = wet[0:1, :]
    rows = [
        head_wet * particular[0:1, :],
        head_wet * from_left[0:1, :],
        head_wet * from_right[0:1, :],
        weight[length - 1:length, :],
        from_left[length - 1:length, :],
        from_right[length - 1:length, :],
        particular[length - 1:length, :],
    ]
    for copy in range(edge_out.shape[0]):
        for k, row in enumerate(rows):
            edge_out[copy, k:k + 1, :] = row


def lon_pass(source, kappa_lon, sea_mask, devices):
    shape = source.shape
    full = jax.ShapeDtypeStruct(shape, jnp.float32)
    edge = jax.ShapeDtypeStruct((devices, TERMS, shape[0] * shape[1]), jnp.float32)
    return pl.pallas_call(lon_kernel, out_shape=(full, full, full, edge))(source, kappa_lon, sea_mask)


def lat_matrix_kernel(kappa_ref, mask_ref, lon_kappa_ref, u_out, w_out, edge_out, scale_out,
                      weight_scratch):
    axis = 1
    wet, weight, position, left_face, right_face = lat_faces(kappa_ref, mask_ref, axis)
    lat_kappa = kappa_ref[...].astype(jnp.float32)
    scale_out[...] = wet * 4.0 * jnp.sqrt(jnp.sqrt(lon_kappa_ref[...].astype(jnp.float32) * lat_kappa))
    shape = wet.shape
    length = shape[axis]
    from_left, from_right = block_solve(
        -left_face,
        -right_face,
        jnp.ones(shape, jnp.float32),
        [jnp.where(position == 0, 1.0, 0.0), jnp.where(position == length - 1, 1.0, 0.0)],
        axis,
    )
    u_out[...] = from_left
    w_out[...] = from_right
    weight_scratch[...] = weight
    head_wet = mask_ref[:, 0, :].astype(jnp.float32)
    edge_out[0] = head_wet * u_out[:, 0, :]
    edge_out[1] = head_wet * w_out[:, 0, :]
    edge_out[2] = weight_scratch[:, length - 1, :]
    edge_out[3] = u_out[:, length - 1, :]
    edge_out[4] = w_out[:, length - 1, :]


def lat_faces(kappa_ref, mask_ref, axis):
    wet = mask_ref[...].astype(jnp.float32)
    weight = kappa_ref[...].astype(jnp.float32) * wet
    position = lax.broadcasted_iota(jnp.int32, wet.shape, axis)
    last = position == wet.shape[axis] - 1
    right_face = jnp.where(last, 0.0, weight * shifted(wet, -1, axis))
    left_face = shifted(right_face, 1, axis)
    return wet, weight, position, left_face, right_face


def lat_rhs_kernel(index_ref, gathered_ref, p_ref, u_ref, w_ref, kappa_ref, mask_ref,
                   matrix_edge_ref, p_out, edge_out):
    axis = 1
    terms = [gathered_ref[:, k, :] for k in range(TERMS)]
    flux = flux_system(terms, True, lambda values, shift, along: shifted(values, shift, along))
    devices, lines = flux.shape
    device = lax.broadcasted_iota(jnp.int32, flux.shape, 0)
    index = index_ref[0]

    def pick(place):
        return jnp.sum(jnp.where(device == place, flux, 0.0), axis=0, keepdims=True)

    levels, rows, width = p_ref.shape
    padded = jnp.concatenate(
        [
            pick((index + devices - 1) % devices),
            pick(index),
            jnp.zeros((width - 2, lines), jnp.float32),
        ],
        0,
    )
    columns = jnp.transpose(padded)
    before = columns[:, 0:1].reshape(levels, rows, 1)
    here = columns[:, 1:2].reshape(levels, rows, 1)
    values = p_ref[...] - u_ref[...] * before + w_ref[...] * here
    wet, weight, position, left_face, right_face = lat_faces(kappa_ref, mask_ref, axis)
    (particular,) = block_solve(
        -left_face, -right_face, jnp.ones(values.shape, jnp.float32), [values], axis
    )
    p_out[...] = particular
    length = values.shape[axis]
    edge_out[0] = mask_ref[:, 0, :].astype(jnp.float32) * p_out[:, 0, :]
    edge_out[1:TERMS - 1] = matrix_edge_ref[...]
    edge_out[TERMS - 1] = p_out[:, length - 1, :]


def lat_matrix(kappa_lat, sea_mask, kappa_lon):
    shape = kappa_lat.shape
    full = jax.ShapeDtypeStruct(shape, jnp.float32)
    edge = jax.ShapeDtypeStruct((TERMS - 2, shape[0], shape[2]), jnp.float32)
    return pl.pallas_call(
        lat_matrix_kernel,
        out_shape=(full, full, edge, full),
        scratch_shapes=[pltpu.VMEM(shape, jnp.float32)],
    )(kappa_lat, sea_mask, kappa_lon)


def lat_rhs(gathered, *inputs):
    shape = inputs[0].shape
    index = jnp.full((1,), lax.axis_index("lon"), jnp.int32)
    vmem = pl.BlockSpec(memory_space=pltpu.VMEM)
    return pl.pallas_call(
        lat_rhs_kernel,
        out_shape=(
            jax.ShapeDtypeStruct(shape, jnp.float32),
            jax.ShapeDtypeStruct((TERMS, shape[0], shape[2]), jnp.float32),
        ),
        in_specs=[pl.BlockSpec(memory_space=pltpu.SMEM)] + [vmem] * (1 + len(inputs)),
        out_specs=(vmem, vmem),
    )(index, gathered, *inputs)


def circular_solve(lower_band, upper_band, excess, sources, roll=jnp.roll):
    devices = lower_band.shape[0]
    stride = 1
    while stride < devices:
        inverse = 1.0 / (excess - lower_band - upper_band)
        left_weight = -lower_band * roll(inverse, stride, 0)
        right_coefficient = -upper_band * roll(inverse, -stride, 0)
        new_lower = left_weight * roll(lower_band, stride, 0)
        new_upper = right_coefficient * roll(upper_band, -stride, 0)
        excess = (
            excess
            + left_weight * roll(excess, stride, 0)
            + right_coefficient * roll(excess, -stride, 0)
        )
        sources = (
            sources
            + left_weight * roll(sources, stride, 0)
            + right_coefficient * roll(sources, -stride, 0)
        )
        lower_band, upper_band = (new_lower, new_upper)
        stride = stride * 2
    return sources / excess


def flux_system(terms, periodic, roll=jnp.roll):
    head_p, head_u, head_w, tail_kappa, tail_u, tail_w, tail_p = terms
    devices = head_p.shape[0]

    def next_of(member):
        return roll(member, -1, 0)

    next_wet = jnp.where(next_of(head_u) > 0.0, 1.0, 0.0)
    face = tail_kappa * next_wet
    if not periodic:
        device = lax.broadcasted_iota(jnp.int32, face.shape, 0)
        face = jnp.where(device == devices - 1, 0.0, face)
        tail_kappa = jnp.where(device == devices - 1, 0.0, tail_kappa)
    lower = -face * tail_u
    upper = -tail_kappa * next_of(head_w)
    diagonal = 1.0 + tail_kappa * next_of(head_u) + face * tail_w
    if not periodic:
        sources = tail_kappa * next_of(head_p) - face * tail_p
        ratios, reduced = [], []
        for place in range(devices):
            pivot = diagonal[place]
            source = sources[place]
            if place > 0:
                pivot = pivot - lower[place] * ratios[-1]
                source = source - lower[place] * reduced[-1]
            ratios.append(upper[place] / pivot)
            reduced.append(source / pivot)
        solved = [reduced[-1]]
        for place in range(devices - 2, -1, -1):
            solved.append(reduced[place] - ratios[place] * solved[-1])
        return jnp.stack(solved[::-1], 0)
    return circular_solve(
        lower, upper, diagonal + lower + upper, tail_kappa * next_of(head_p) - face * tail_p, roll
    )


def interface_flux(edge, axis, mesh_axis, periodic, exchange):
    terms = lax.slice_in_dim(edge, 0, TERMS, axis=axis) if edge.shape[axis] > TERMS else edge
    devices = lax.axis_size(mesh_axis)
    if exchange == "all_to_all":
        copies = jnp.broadcast_to(terms[None], (devices,) + terms.shape)
        gathered = lax.all_to_all(copies, mesh_axis, 0, 0, tiled=True)
    else:
        gathered = lax.all_gather(terms[None], mesh_axis, axis=0, tiled=True)
    terms = [lax.index_in_dim(gathered, k, axis + 1, keepdims=False) for k in range(TERMS)]
    flux = flux_system(terms, periodic)
    index = lax.axis_index(mesh_axis)
    here = lax.dynamic_index_in_dim(flux, index, 0, keepdims=True)
    before = lax.dynamic_index_in_dim(flux, (index + devices - 1) % devices, 0, keepdims=True)
    return before[0], here[0]


def lon_flux(copies):
    devices = copies.shape[0]
    gathered = lax.all_to_all(copies, "lon", 0, 0, tiled=True)
    terms = [gathered[:, k] for k in range(TERMS)]
    flux = flux_system(terms, True)
    index = lax.axis_index("lon")
    here = lax.dynamic_index_in_dim(flux, index, 0, keepdims=False)
    before = lax.dynamic_index_in_dim(flux, (index + devices - 1) % devices, 0, keepdims=False)
    return before, here


def shards(source, kappa_lon, kappa_lat, sea_mask):
    p_lon, u_lon, w_lon, edge_lon = lon_pass(source, kappa_lon, sea_mask, lax.axis_size("lon"))
    u_lat, w_lat, matrix_edge, scale = lat_matrix(kappa_lat, sea_mask, kappa_lon)
    gathered = lax.all_to_all(edge_lon, "lon", 0, 0, tiled=True)
    p_lat, edge_lat = lat_rhs(
        gathered, p_lon, u_lon, w_lon, kappa_lat, sea_mask, matrix_edge,
    )
    before, here = interface_flux(edge_lat, 0, "lat", False, "all_gather")
    return scale * (p_lat - u_lat * before[:, None, :] + w_lat * here[:, None, :])


def solution(mesh):
    return jax.shard_map(
        shards,
        mesh=mesh,
        in_specs=(
            P(None, "lat", "lon"),
            P(None, "lat", "lon"),
            P(None, "lat", "lon"),
            P(None, "lat", "lon"),
        ),
        out_specs=P(None, "lat", "lon"),
        check_vma=False,
    )
```
